128 devices in a mesh: kv: 2 (over core), page: 64 (over z, y, x).
Axes of the slice: x: 4, y: 4, z: 4, core: 2. Of those that a mesh axis runs over, the one named last changes fastest.
Arguments:
- tokens: bfloat16 [16384, 2048], P('page'), may hold values from -6 to 6
- in_gain: float32 [2048], replicated, may hold values from 0.4 to 1.6
- w_query: bfloat16 [2048, 2048], P(None, 'kv'), may hold values from -0.125 to 0.125
- key_projection_weight: bfloat16 [2048, 512], P(None, 'kv'), may hold values from -0.125 to 0.125
- value_projection_weight: bfloat16 [2048, 512], P(None, 'kv'), may hold values from -0.125 to 0.125
- q_gain: float32 [256], replicated, may hold values from 0.5 to 6
- k_gain: float32 [256], replicated, may hold values from 0.4 to 1.6
- w_out: bfloat16 [2048, 2048], P('kv'), may hold values from -0.125 to 0.125
- post_gain: float32 [2048], replicated, may hold values from 0.25 to 1.75
- laurel_left: bfloat16 [2048, 64], replicated, may hold values from -0.125 to 0.125
- laurel_right: bfloat16 [64, 2048], replicated, may hold values from -0.75 to 0.75
- laurel_gain: float32 [2048], replicated, may hold values from 0.25 to 1.75
- prefix_key_slots: bfloat16 [16384, 512], P('page', 'kv'), may hold values from -20 to 20
- prefix_value_slots: bfloat16 [16384, 512], P('page', 'kv'), may hold values from -6 to 6
- prefix_slot_map: int32 [128], replicated, may hold values from 0 to 127, each once
- page_lengths: int32 [32], replicated, may hold values from 1 to 8, 128 in all
- request_group: int32 [32], replicated, may hold values from 0 to 3
- suffix_page_map: int32 [128], P('page'), may hold values from 0 to 127, as said below
Outputs:
- layer_out: bfloat16 [16384, 2048], P('page', 'kv')
- suffix_key_cache: bfloat16 [16384, 512], P('page', 'kv')
- suffix_value_cache: bfloat16 [16384, 512], P('page', 'kv')
The draws below stay inside these ranges and needn't reach their ends.
Inputs may be any that keep to these rules, and one draw needn't show every extreme that they name: `prefix_slot_map`: A permutation: entry g * 32 + j names the page slot (rows of 128 tokens of prefix_key_slots and prefix_value_slots) that holds page j of prefix g. `page_lengths`: they sum to 128; some request has exactly 8 pages. `suffix_page_map`: A permutation that keeps every logical page within the aligned block of 2 pages that contains it.
All inputs are finite; a program needn't handle non-finite values.
Results may differ from the reference program's by a relative error of at most 0.01.
The reference program's roundings to bfloat16 on the way count: a program that leaves them out, or rounds other values in their place, can miss the bound.
Values may be sent and summed in bfloat16 or wider, within the bound.
No kernel may reach another device: no remote copies, remote signals or barrier semaphores. Data moves between devices by JAX's collectives and lax.ppermute only.
A program may use at most 128 MiB of HBM per device.

```python
import math
import jax
import jax.numpy as jnp
import numpy as np
from jax import lax

MODEL_DIM = 2048
QUERY_HEADS = 8
KEY_VALUE_HEADS = 2
HEAD_SIZE = 256
RANK = 64
PAGE_TOKENS = 128
PREFIX_TOKENS = 4096
PREFIX_COUNT = 4
MAXP = 8
PAGES_DEV = 2
PREFIX_PAGES = 32
SUFFIX_PAGES = 128
SUFFIX_TOKENS = 16384
REQS = 32


def draw_q_gain(key, part):
    return jax.random.uniform(key, (HEAD_SIZE,), jnp.float32, 0.5, 1.5)


def draw_prefix_key_slots(key, part):
    start_offset = jax.random.normal(jax.random.fold_in(key, 11), (PREFIX_COUNT * PREFIX_TOKENS, KEY_VALUE_HEADS * HEAD_SIZE), jnp.float32)
    start_offset = jnp.clip(start_offset, -6.0, 6.0)
    column_scale_factor = jax.random.uniform(jax.random.fold_in(key, 13), (1, KEY_VALUE_HEADS * HEAD_SIZE), jnp.float32, 0.4, 1.6)
    start_offset = start_offset * column_scale_factor
    return start_offset.astype(jnp.bfloat16)


def draw_suffix_page_map(key, part):
    blocks = SUFFIX_PAGES // PAGES_DEV
    block_keys = jax.random.split(jax.random.fold_in(key, 21), blocks)
    orders = jax.vmap(lambda block_key: jax.random.permutation(block_key, PAGES_DEV))(block_keys)
    return (orders + (jnp.arange(blocks) * PAGES_DEV)[:, None]).reshape(SUFFIX_PAGES).astype(jnp.int32)


def plant(drawn, key, smallest, high):
    index_at = [jax.random.randint(jax.random.fold_in(key, axis), (), 0, length) for axis, length in enumerate(drawn.shape)]
    widest = drawn.shape.index(max(drawn.shape))
    neighbour = index_at[:widest] + [(index_at[widest] + 1) % drawn.shape[widest]] + index_at[widest + 1:]
    return drawn.at[tuple(index_at)].set(smallest).at[tuple(neighbour)].set(high)


def shard_levels(key, extent, shards, least, largest):
    loudness = 1.0
    for axis_at, blocks in shards:
        draws = jax.random.uniform(jax.random.fold_in(jax.random.fold_in(key, 6), axis_at), (blocks,), jnp.float32, least / len(shards), largest / len(shards))
        loudness = loudness * jnp.repeat(jnp.exp(draws), extent[axis_at] // blocks).reshape((-1,) + (1,) * (len(extent) - 1 - axis_at))
    return loudness


def split_up(count, total, limit, slope):
    portions = [(1 << 20) // math.isqrt(rank ** slope) + 1 for rank in range(2, count + 1)]
    surplus, counts = total - limit - (count - 1), [1] * (count - 1)
    while surplus > 0:
        free = [i for i in range(count - 1) if counts[i] < limit]
        whole, remaining = sum([portions[i] for i in free]), surplus
        for i in free:
            extra = min(limit - counts[i], max(1, remaining * portions[i] // whole), surplus)
            counts[i] = counts[i] + extra
            surplus = surplus - extra
    return np.array([limit] + counts)


def uneven(stream_key, count, total, bound, skew):
    if count == 2:
        one = jax.random.randint(stream_key, (), max(1, total - bound), min(bound, total - 1) + 1)
        return jnp.stack([one, total - one])
    lengths = jnp.asarray(split_up(count, total, bound, skew), jnp.int32)
    pairs = (count - 1) // 2
    source_of, sink = lengths[1:1 + 2 * pairs:2], lengths[2:2 + 2 * pairs:2]
    room = jnp.minimum(source_of - 1, bound - sink)
    shifted = jax.random.randint(jax.random.fold_in(stream_key, 1), (pairs,), 0, 1 << 20) % (room + 1)
    lengths = lengths.at[1:1 + 2 * pairs:2].set(source_of - shifted).at[2:2 + 2 * pairs:2].set(sink + shifted)
    return lengths[jax.random.permutation(jax.random.fold_in(stream_key, 2), count)]


def normal_values(own_key, extent, deviation, reach, cuts=(), kind=jnp.bfloat16):
    array = deviation * jax.random.normal(own_key, extent, jnp.float32)
    if cuts:
        array = array * shard_levels(own_key, extent, cuts, -0.22, 0.18)
    return jnp.clip(array, -reach, reach).astype(kind)


def setup_inputs(seed: int = 0) -> dict:
    key_of = jax.random.split(jax.random.key(seed), 19)
    tokens = normal_values(key_of[0], (SUFFIX_TOKENS, MODEL_DIM), 1.0, 6.0, ((0, 64),))
    in_gain = jnp.clip(1.0 + 0.12 * jax.random.normal(key_of[1], (MODEL_DIM,), jnp.float32), 0.4, 1.6)
    w_query = normal_values(key_of[2], (MODEL_DIM, QUERY_HEADS * HEAD_SIZE), MODEL_DIM ** -0.5, 0.125, ((1, 2),))
    key_projection_weight = normal_values(key_of[3], (MODEL_DIM, KEY_VALUE_HEADS * HEAD_SIZE), MODEL_DIM ** -0.5, 0.125, ((1, 2),))
    value_projection_weight = normal_values(key_of[4], (MODEL_DIM, KEY_VALUE_HEADS * HEAD_SIZE), MODEL_DIM ** -0.5, 0.125, ((1, 2),))
    q_gain = draw_q_gain(jax.random.fold_in(key_of[18], 71), 0)
    k_gain = jnp.clip(1.0 + 0.12 * jax.random.normal(key_of[6], (HEAD_SIZE,), jnp.float32), 0.4, 1.6)
    w_out = normal_values(key_of[7], (QUERY_HEADS * HEAD_SIZE, MODEL_DIM), (QUERY_HEADS * HEAD_SIZE) ** -0.5, 0.125, ((0, 2),))
    post_gain = jnp.clip(1.0 + 0.15 * jax.random.normal(key_of[8], (MODEL_DIM,), jnp.float32), 0.25, 1.75)
    laurel_left = normal_values(key_of[9], (MODEL_DIM, RANK), MODEL_DIM ** -0.5, 0.125)
    laurel_right = normal_values(key_of[10], (RANK, MODEL_DIM), RANK ** -0.5, 0.75)
    laurel_gain = jnp.clip(1.0 + 0.15 * jax.random.normal(key_of[11], (MODEL_DIM,), jnp.float32), 0.25, 1.75)
    prefix_key_slots = draw_prefix_key_slots(jax.random.fold_in(key_of[18], 71), 0)
    prefix_value_slots = normal_values(key_of[13], (PREFIX_COUNT * PREFIX_TOKENS, KEY_VALUE_HEADS * HEAD_SIZE), 1.0, 6.0, ((0, 64), (1, 2)))
    prefix_slot_map = jax.random.permutation(key_of[14], PREFIX_COUNT * PREFIX_PAGES).astype(jnp.int32)
    page_lengths = uneven(key_of[15], REQS, SUFFIX_PAGES, MAXP, 2).astype(jnp.int32)
    request_group = plant(jax.random.randint(key_of[16], (REQS,), 0, PREFIX_COUNT), jax.random.fold_in(key_of[16], 1), 0, PREFIX_COUNT - 1).astype(jnp.int32)
    suffix_page_map = draw_suffix_page_map(jax.random.fold_in(key_of[18], 71), 0)
    return {"tokens": tokens, "in_gain": in_gain, "w_query": w_query, "key_projection_weight": key_projection_weight, "value_projection_weight": value_projection_weight, "q_gain": q_gain, "k_gain": k_gain, "w_out": w_out, "post_gain": post_gain, "laurel_left": laurel_left, "laurel_right": laurel_right, "laurel_gain": laurel_gain, "prefix_key_slots": prefix_key_slots, "prefix_value_slots": prefix_value_slots, "prefix_slot_map": prefix_slot_map, "page_lengths": page_lengths, "request_group": request_group, "suffix_page_map": suffix_page_map}


epsilon = 1e-06
rope_base = 1000000.0
masked_low = -1e+30

def rms_scale(values):
    return lax.rsqrt(lax.optimization_barrier(jnp.mean(values * values, axis=-1, keepdims=True)) + epsilon)

def rotate(values, positions):
    half_dim = values.shape[-1] // 2
    inv_freq = rope_base ** (-(jnp.arange(half_dim).astype(jnp.float32) * 2.0 / values.shape[-1]))
    angles = positions.astype(jnp.float32)[:, None] * inv_freq[None, :]
    cosine = jnp.cos(angles)[:, None, :]
    sines = jnp.sin(angles)[:, None, :]
    first_half = values[..., :half_dim]
    second_half = values[..., half_dim:]
    return jnp.concatenate([first_half * cosine - second_half * sines, second_half * cosine + first_half * sines], axis=-1)

def project(tokens, in_gain, w_query, key_projection_weight, value_projection_weight, q_gain, k_gain, positions):
    tok_count = tokens.shape[0]
    tokens_wide = tokens.astype(jnp.float32)
    normed = (tokens_wide * rms_scale(tokens_wide) * in_gain).astype(jnp.bfloat16)
    queries = jnp.dot(normed, w_query, preferred_element_type=jnp.float32).reshape(tok_count, -1, HEAD_SIZE)
    queries = rotate(queries * rms_scale(queries) * q_gain, positions).astype(jnp.bfloat16)
    fresh_key_rows = jnp.dot(normed, key_projection_weight, preferred_element_type=jnp.float32).reshape(tok_count, -1, HEAD_SIZE)
    fresh_key_rows = rotate(fresh_key_rows * rms_scale(fresh_key_rows) * k_gain, positions).astype(jnp.bfloat16)
    fresh_value_rows = jnp.dot(normed, value_projection_weight, preferred_element_type=jnp.float32).reshape(tok_count, -1, HEAD_SIZE)
    fresh_value_rows = (fresh_value_rows * rms_scale(fresh_value_rows)).astype(jnp.bfloat16)
    return (normed, queries, fresh_key_rows, fresh_value_rows)

def reference(tokens, in_gain, w_query, key_projection_weight, value_projection_weight, q_gain, k_gain, w_out, post_gain, laurel_left, laurel_right, laurel_gain, prefix_key_slots, prefix_value_slots, prefix_slot_map, page_lengths, request_group, suffix_page_map):
    tok_ids = jnp.arange(SUFFIX_TOKENS, dtype=jnp.int32)
    page_starts = (jnp.cumsum(page_lengths) - page_lengths).astype(jnp.int32)
    page_of = tok_ids // PAGE_TOKENS
    belongs = ((page_of[:, None] >= page_starts[None, :]) & (page_of[:, None] < (page_starts + page_lengths)[None, :])).astype(jnp.int32)
    positions = (PREFIX_TOKENS + tok_ids - lax.optimization_barrier(jnp.sum(belongs * page_starts[None, :], axis=1)) * PAGE_TOKENS).astype(jnp.int32)
    normed, queries, fresh_key_rows, fresh_value_rows = project(tokens, in_gain, w_query, key_projection_weight, value_projection_weight, q_gain, k_gain, positions)
    sliding_window_rows = MAXP * PAGE_TOKENS
    padded_query = jnp.concatenate([queries, jnp.zeros((sliding_window_rows, QUERY_HEADS, HEAD_SIZE), jnp.bfloat16)], axis=0)
    key_with_padding = jnp.concatenate([fresh_key_rows, jnp.zeros((sliding_window_rows, KEY_VALUE_HEADS, HEAD_SIZE), jnp.bfloat16)], axis=0)
    value_with_padding = jnp.concatenate([fresh_value_rows, jnp.zeros((sliding_window_rows, KEY_VALUE_HEADS, HEAD_SIZE), jnp.bfloat16)], axis=0)
    key_by_group = prefix_key_slots.reshape(PREFIX_COUNT * PREFIX_PAGES, PAGE_TOKENS, KEY_VALUE_HEADS, HEAD_SIZE)[prefix_slot_map].reshape(PREFIX_COUNT, PREFIX_TOKENS, KEY_VALUE_HEADS, HEAD_SIZE)
    value_by_group = prefix_value_slots.reshape(PREFIX_COUNT * PREFIX_PAGES, PAGE_TOKENS, KEY_VALUE_HEADS, HEAD_SIZE)[prefix_slot_map].reshape(PREFIX_COUNT, PREFIX_TOKENS, KEY_VALUE_HEADS, HEAD_SIZE)

    def one_request(outputs, request_item):
        begin_page, page_count, group_id = request_item
        row_begin = (begin_page * PAGE_TOKENS).astype(jnp.int32)
        query_block_rows = lax.dynamic_slice_in_dim(padded_query, row_begin, sliding_window_rows, 0)
        block_key = lax.dynamic_slice_in_dim(key_with_padding, row_begin, sliding_window_rows, 0)
        block_value = lax.dynamic_slice_in_dim(value_with_padding, row_begin, sliding_window_rows, 0)
        group_keys = lax.dynamic_index_in_dim(key_by_group, group_id, 0, keepdims=False)
        group_values = lax.dynamic_index_in_dim(value_by_group, group_id, 0, keepdims=False)
        all_keys = jnp.concatenate([group_keys, block_key], axis=0).astype(jnp.float32)
        all_values = jnp.concatenate([group_values, block_value], axis=0).astype(jnp.float32)
        query_broadened = query_block_rows.astype(jnp.float32).reshape(sliding_window_rows, KEY_VALUE_HEADS, QUERY_HEADS // KEY_VALUE_HEADS, HEAD_SIZE)
        scores = jnp.einsum('qcgd,kcd->qcgk', query_broadened, all_keys)
        local_ids = jnp.arange(sliding_window_rows, dtype=jnp.int32)
        allowed = (local_ids[None, :] <= local_ids[:, None]) & (local_ids[None, :] < page_count * PAGE_TOKENS)
        allowed_keys = jnp.concatenate([jnp.ones((sliding_window_rows, PREFIX_TOKENS), bool), allowed], axis=1)[:, None, None, :]
        scores = jnp.where(allowed_keys, scores, masked_low)
        row_top = lax.optimization_barrier(jnp.max(scores, axis=-1, keepdims=True))
        weights = jnp.where(allowed_keys, jnp.exp(scores - row_top), 0.0)
        row_total = lax.optimization_barrier(jnp.sum(weights, axis=-1))
        rounded = lax.optimization_barrier(weights.astype(jnp.bfloat16)).astype(jnp.float32)
        mixture = jnp.einsum('qcgk,kcd->qcgd', rounded, all_values) / row_total[..., None]
        block_out = mixture.reshape(sliding_window_rows, QUERY_HEADS * HEAD_SIZE).astype(jnp.bfloat16)
        return (lax.dynamic_update_slice_in_dim(outputs, block_out, row_begin, 0), None)
    outputs = jnp.zeros((SUFFIX_TOKENS + sliding_window_rows, QUERY_HEADS * HEAD_SIZE), jnp.bfloat16)
    outputs, unused = lax.scan(one_request, outputs, (page_starts, page_lengths.astype(jnp.int32), request_group.astype(jnp.int32)))
    attended = outputs[:SUFFIX_TOKENS]
    attn_sum = jnp.dot(attended, w_out, preferred_element_type=jnp.float32)
    attn_branch = attn_sum * rms_scale(attn_sum) * post_gain
    low_rank = jnp.dot(normed, laurel_left, preferred_element_type=jnp.float32).astype(jnp.bfloat16)
    laurel_lr = jnp.dot(low_rank, laurel_right, preferred_element_type=jnp.float32)
    laurel = normed.astype(jnp.float32) + laurel_lr * rms_scale(laurel_lr) * laurel_gain
    layer_out = ((tokens.astype(jnp.float32) + attn_branch + laurel) * 2.0 ** (-0.5)).astype(jnp.bfloat16)
    paged_key_rows = fresh_key_rows.reshape(SUFFIX_PAGES, PAGE_TOKENS * KEY_VALUE_HEADS * HEAD_SIZE)
    paged_value_rows = fresh_value_rows.reshape(SUFFIX_PAGES, PAGE_TOKENS * KEY_VALUE_HEADS * HEAD_SIZE)
    suffix_key_cache = jnp.zeros_like(paged_key_rows).at[suffix_page_map].set(paged_key_rows).reshape(SUFFIX_TOKENS, KEY_VALUE_HEADS * HEAD_SIZE)
    suffix_value_cache = jnp.zeros_like(paged_value_rows).at[suffix_page_map].set(paged_value_rows).reshape(SUFFIX_TOKENS, KEY_VALUE_HEADS * HEAD_SIZE)
    return (layer_out, suffix_key_cache, suffix_value_cache)
```

```python
import jax
import jax.numpy as jnp
from jax import lax
from jax.sharding import PartitionSpec as P

HEAD_SIZE = 256
PAGE_TOKENS = 128
PREFIX_TOKENS = 4096
PREFIX_COUNT = 4
MAXP = 8
PREFIX_PAGES = 32


epsilon = 1e-06
rope_base = 1000000.0
masked_low = -1e30


def passed_along(block, axis, distance):
    devices = range(lax.axis_size(axis))
    route = [(i - distance, i) for i in devices if i - distance in devices]
    return lax.ppermute(block, axis, route)


def rms_scale(values):
    return lax.rsqrt(jnp.mean(values * values, axis=-1, keepdims=True) + epsilon)


def rotate(values, positions):
    half_dim = values.shape[-1] // 2
    inv_freq = rope_base ** (-(jnp.arange(half_dim).astype(jnp.float32) * 2.0 / values.shape[-1]))
    angles = positions.astype(jnp.float32)[:, None] * inv_freq[None, :]
    cosine = jnp.cos(angles)[:, None, :]
    sines = jnp.sin(angles)[:, None, :]
    first_half = values[..., :half_dim]
    second_half = values[..., half_dim:]
    return jnp.concatenate(
        [first_half * cosine - second_half * sines, second_half * cosine + first_half * sines],
        axis=-1,
    )


def project(
    tokens,
    in_gain,
    w_query,
    key_projection_weight,
    value_projection_weight,
    q_gain,
    k_gain,
    positions,
):
    tok_count = tokens.shape[0]
    tokens_wide = tokens.astype(jnp.float32)
    normed = (tokens_wide * rms_scale(tokens_wide) * in_gain).astype(jnp.bfloat16)
    queries = jnp.dot(normed, w_query, preferred_element_type=jnp.float32).reshape(
        tok_count, -1, HEAD_SIZE
    )
    queries = rotate(queries * rms_scale(queries) * q_gain, positions).astype(jnp.bfloat16)
    fresh_key_rows = jnp.dot(
        normed, key_projection_weight, preferred_element_type=jnp.float32
    ).reshape(tok_count, -1, HEAD_SIZE)
    fresh_key_rows = rotate(fresh_key_rows * rms_scale(fresh_key_rows) * k_gain, positions).astype(
        jnp.bfloat16
    )
    fresh_value_rows = jnp.dot(
        normed, value_projection_weight, preferred_element_type=jnp.float32
    ).reshape(tok_count, -1, HEAD_SIZE)
    fresh_value_rows = (fresh_value_rows * rms_scale(fresh_value_rows)).astype(jnp.bfloat16)
    return (
        normed,
        queries,
        fresh_key_rows.reshape(tok_count, HEAD_SIZE),
        fresh_value_rows.reshape(tok_count, HEAD_SIZE),
    )


def token_places(first_index, tok_count, page_lengths, request_group):
    tok_ids = first_index + jnp.arange(tok_count, dtype=jnp.int32)
    page_of = tok_ids // PAGE_TOKENS
    page_starts = jnp.cumsum(page_lengths) - page_lengths
    belongs = (page_of[:, None] >= page_starts[None, :]) & (
        page_of[:, None] < (page_starts + page_lengths)[None, :]
    )
    belongs = (belongs & (tok_ids[:, None] >= 0)).astype(jnp.int32)
    request_ids = jnp.arange(page_starts.shape[0], dtype=jnp.int32)
    requests = jnp.sum(belongs * request_ids[None, :], axis=1) - (1 - jnp.sum(belongs, axis=1))
    position = tok_ids - jnp.sum(belongs * page_starts[None, :], axis=1) * PAGE_TOKENS
    groups = jnp.sum(belongs * request_group[None, :], axis=1)
    return (requests, position, groups)


def attend(queries, keys_block, values_block, key_mask):
    scores = jnp.einsum("qhd,kd->qhk", queries, keys_block, preferred_element_type=jnp.float32)
    wide_mask = key_mask[:, None, :]
    scores = jnp.where(wide_mask, scores, masked_low)
    row_top = jnp.max(scores, axis=-1)
    weights = jnp.where(wide_mask, jnp.exp(scores - row_top[..., None]), 0.0)
    row_total = jnp.sum(weights, axis=-1)
    mixture = jnp.einsum(
        "qhk,kd->qhd",
        weights.astype(jnp.bfloat16),
        values_block,
        preferred_element_type=jnp.float32,
    )
    return (row_top, row_total, mixture)


def combine(carried, incoming):
    row_top = jnp.maximum(carried[0], incoming[0])
    old_factor = jnp.exp(carried[0] - row_top)
    new_factor = jnp.exp(incoming[0] - row_top)
    row_total = carried[1] * old_factor + incoming[1] * new_factor
    mixture = carried[2] * old_factor[..., None] + incoming[2] * new_factor[..., None]
    return (row_top, row_total, mixture)


def local(
    tokens,
    in_gain,
    w_query,
    key_projection_weight,
    value_projection_weight,
    q_gain,
    k_gain,
    w_out,
    post_gain,
    laurel_left,
    laurel_right,
    laurel_gain,
    prefix_key_slots,
    prefix_value_slots,
    prefix_slot_map,
    page_lengths,
    request_group,
    suffix_page_map,
):
    tok_count = tokens.shape[0]
    pages_here = tok_count // PAGE_TOKENS
    device = lax.axis_index("page")
    first_index = device * tok_count
    prefix_both = jnp.concatenate([prefix_key_slots, prefix_value_slots], axis=1)
    every_slot = lax.all_gather(prefix_both, "page", axis=0, tiled=True)
    requests, position, groups = token_places(first_index, tok_count, page_lengths, request_group)
    normed, queries, fresh_key_rows, fresh_value_rows = project(
        tokens,
        in_gain,
        w_query,
        key_projection_weight,
        value_projection_weight,
        q_gain,
        k_gain,
        position + PREFIX_TOKENS,
    )
    local_slot = suffix_page_map - device * pages_here
    placing = (local_slot[:, None] == jnp.arange(pages_here, dtype=jnp.int32)[None, :]).astype(
        jnp.bfloat16
    )
    both_pages = jnp.concatenate(
        [
            fresh_key_rows.reshape(pages_here, PAGE_TOKENS * HEAD_SIZE),
            fresh_value_rows.reshape(pages_here, PAGE_TOKENS * HEAD_SIZE),
        ],
        axis=1,
    )
    placed = jnp.dot(placing.T, both_pages, preferred_element_type=jnp.float32).astype(jnp.bfloat16)
    suffix_key_cache = placed[:, : PAGE_TOKENS * HEAD_SIZE].reshape(tok_count, HEAD_SIZE)
    suffix_value_cache = placed[:, PAGE_TOKENS * HEAD_SIZE :].reshape(tok_count, HEAD_SIZE)

    reach = (MAXP + pages_here - 2) // pages_here
    fresh_both = jnp.concatenate([fresh_key_rows, fresh_value_rows], axis=1)
    window = fresh_both
    covered = 1
    while covered < reach + 1:
        step = min(covered, reach + 1 - covered)
        moved = passed_along(window[: step * tok_count], "page", covered)
        window = jnp.concatenate([window, moved], axis=0)
        covered += step
    window_requests = []
    window_positions = []
    for shift_step in range(reach + 1):
        far_requests, far_position, _ = token_places(
            first_index - shift_step * tok_count, tok_count, page_lengths, request_group
        )
        window_requests.append(far_requests)
        window_positions.append(far_position)
    key_requests = jnp.concatenate(window_requests, axis=0)
    key_positions = jnp.concatenate(window_positions, axis=0)
    suffix_keys = window[:, :HEAD_SIZE]
    suffix_values = window[:, HEAD_SIZE:]

    heads = queries.shape[1]
    page_queries = queries.reshape(pages_here, PAGE_TOKENS, heads, HEAD_SIZE)
    page_requests = requests.reshape(pages_here, PAGE_TOKENS)
    page_positions = position.reshape(pages_here, PAGE_TOKENS)
    page_groups = groups.reshape(pages_here, PAGE_TOKENS)[:, 0]
    chosen = jnp.take(
        prefix_slot_map.reshape(PREFIX_COUNT, PREFIX_PAGES), page_groups, axis=0
    )
    slot_pages = every_slot.reshape(-1, PAGE_TOKENS, 2 * HEAD_SIZE)
    group_rows = jnp.take(slot_pages, chosen.reshape(-1), axis=0).reshape(
        pages_here, PREFIX_PAGES * PAGE_TOKENS, 2 * HEAD_SIZE
    )
    prefix_keys = group_rows[..., :HEAD_SIZE]
    prefix_values = group_rows[..., HEAD_SIZE:]
    prefix_scores = jnp.einsum(
        "pqhd,pkd->pqhk", page_queries, prefix_keys, preferred_element_type=jnp.float32
    )
    suffix_scores = jnp.einsum(
        "pqhd,kd->pqhk", page_queries, suffix_keys, preferred_element_type=jnp.float32
    )
    suffix_mask = (page_requests[:, :, None] == key_requests[None, None, :]) & (
        key_positions[None, None, :] <= page_positions[:, :, None]
    )
    suffix_mask = suffix_mask[:, :, None, :]
    suffix_scores = jnp.where(suffix_mask, suffix_scores, masked_low)
    row_top = jnp.maximum(
        jnp.max(prefix_scores, axis=-1), jnp.max(suffix_scores, axis=-1)
    )[..., None]
    prefix_weights = jnp.exp(prefix_scores - row_top)
    suffix_weights = jnp.where(suffix_mask, jnp.exp(suffix_scores - row_top), 0.0)
    row_total = jnp.sum(prefix_weights, axis=-1) + jnp.sum(suffix_weights, axis=-1)
    mixture = jnp.einsum(
        "pqhk,pkd->pqhd",
        prefix_weights.astype(jnp.bfloat16),
        prefix_values,
        preferred_element_type=jnp.float32,
    ) + jnp.einsum(
        "pqhk,kd->pqhd",
        suffix_weights.astype(jnp.bfloat16),
        suffix_values,
        preferred_element_type=jnp.float32,
    )
    attended = (mixture / row_total[..., None]).astype(jnp.bfloat16).reshape(tok_count, -1)
    attn_part = jnp.dot(attended, w_out, preferred_element_type=jnp.float32)
    kv_index = lax.axis_index("kv")
    model_width = tokens.shape[1]
    half_width = model_width // lax.axis_size("kv")

    def columns(source):
        return lax.dynamic_slice_in_dim(source, kv_index * half_width, half_width, source.ndim - 1)

    partner_part = lax.ppermute(attn_part.astype(jnp.bfloat16), "kv", [(0, 1), (1, 0)])
    summed_out = attn_part + partner_part.astype(jnp.float32)
    low_rank = jnp.dot(normed, laurel_left, preferred_element_type=jnp.float32).astype(jnp.bfloat16)
    laurel_full = jnp.dot(low_rank, laurel_right, preferred_element_type=jnp.float32)
    attn_half = columns(summed_out)
    attn_branch = attn_half * rms_scale(summed_out) * columns(post_gain)
    laurel = columns(normed).astype(jnp.float32) + columns(laurel_full) * rms_scale(
        laurel_full
    ) * columns(laurel_gain)
    layer_out = (
        (columns(tokens).astype(jnp.float32) + attn_branch + laurel) * 2.0 ** (-0.5)
    ).astype(jnp.bfloat16)
    return (layer_out, suffix_key_cache, suffix_value_cache)


def solution(mesh):
    placed = (
        P("page", None),
        P(),
        P(None, "kv"),
        P(None, "kv"),
        P(None, "kv"),
        P(),
        P(),
        P("kv", None),
        P(),
        P(),
        P(),
        P(),
        P("page", "kv"),
        P("page", "kv"),
        P(),
        P(),
        P(),
        P("page"),
    )
    return jax.shard_map(
        local,
        mesh=mesh,
        in_specs=placed,
        out_specs=(P("page", "kv"), P("page", "kv"), P("page", "kv")),
        check_vma=False,
    )
```

```python
import jax
import jax.numpy as jnp
from jax import lax
from jax.sharding import PartitionSpec as P
from jax.experimental import pallas as pl
from jax.experimental.pallas import tpu as pltpu

HEAD_SIZE = 256
PAGE_TOKENS = 128
PREFIX_TOKENS = 4096
PREFIX_COUNT = 4
MAXP = 8
PREFIX_PAGES = 32


epsilon = 1e-06
rope_base = 1000000.0
masked_low = -1e30


def passed_along(block, axis, distance):
    devices = range(lax.axis_size(axis))
    route = [(i - distance, i) for i in devices if i - distance in devices]
    return lax.ppermute(block, axis, route)


def rms_scale(values):
    return lax.rsqrt(jnp.mean(values * values, axis=-1, keepdims=True) + epsilon)


def rotate(values, positions):
    half_dim = values.shape[-1] // 2
    inv_freq = rope_base ** (-(jnp.arange(half_dim).astype(jnp.float32) * 2.0 / values.shape[-1]))
    angles = positions.astype(jnp.float32)[:, None] * inv_freq[None, :]
    cosine = jnp.cos(angles)[:, None, :]
    sines = jnp.sin(angles)[:, None, :]
    first_half = values[..., :half_dim]
    second_half = values[..., half_dim:]
    return jnp.concatenate(
        [first_half * cosine - second_half * sines, second_half * cosine + first_half * sines],
        axis=-1,
    )


def project(
    tokens,
    in_gain,
    w_query,
    key_projection_weight,
    value_projection_weight,
    q_gain,
    k_gain,
    positions,
):
    tok_count = tokens.shape[0]
    tokens_wide = tokens.astype(jnp.float32)
    normed = (tokens_wide * rms_scale(tokens_wide) * in_gain).astype(jnp.bfloat16)
    queries = jnp.dot(normed, w_query, preferred_element_type=jnp.float32).reshape(
        tok_count, -1, HEAD_SIZE
    )
    queries = rotate(queries * rms_scale(queries) * q_gain, positions).astype(jnp.bfloat16)
    fresh_key_rows = jnp.dot(
        normed, key_projection_weight, preferred_element_type=jnp.float32
    ).reshape(tok_count, -1, HEAD_SIZE)
    fresh_key_rows = rotate(fresh_key_rows * rms_scale(fresh_key_rows) * k_gain, positions).astype(
        jnp.bfloat16
    )
    fresh_value_rows = jnp.dot(
        normed, value_projection_weight, preferred_element_type=jnp.float32
    ).reshape(tok_count, -1, HEAD_SIZE)
    fresh_value_rows = (fresh_value_rows * rms_scale(fresh_value_rows)).astype(jnp.bfloat16)
    return (
        normed,
        queries,
        fresh_key_rows.reshape(tok_count, HEAD_SIZE),
        fresh_value_rows.reshape(tok_count, HEAD_SIZE),
    )


def token_places(first_index, tok_count, page_lengths, request_group):
    tok_ids = first_index + jnp.arange(tok_count, dtype=jnp.int32)
    page_of = tok_ids // PAGE_TOKENS
    page_starts = jnp.cumsum(page_lengths) - page_lengths
    belongs = (page_of[:, None] >= page_starts[None, :]) & (
        page_of[:, None] < (page_starts + page_lengths)[None, :]
    )
    belongs = (belongs & (tok_ids[:, None] >= 0)).astype(jnp.int32)
    request_ids = jnp.arange(page_starts.shape[0], dtype=jnp.int32)
    requests = jnp.sum(belongs * request_ids[None, :], axis=1) - (1 - jnp.sum(belongs, axis=1))
    position = tok_ids - jnp.sum(belongs * page_starts[None, :], axis=1) * PAGE_TOKENS
    groups = jnp.sum(belongs * request_group[None, :], axis=1)
    return (requests, position, groups)


def attend(queries, keys_block, values_block, key_mask):
    scores = jnp.einsum("qhd,kd->qhk", queries, keys_block, preferred_element_type=jnp.float32)
    wide_mask = key_mask[:, None, :]
    scores = jnp.where(wide_mask, scores, masked_low)
    row_top = jnp.max(scores, axis=-1)
    weights = jnp.where(wide_mask, jnp.exp(scores - row_top[..., None]), 0.0)
    row_total = jnp.sum(weights, axis=-1)
    mixture = jnp.einsum(
        "qhk,kd->qhd",
        weights.astype(jnp.bfloat16),
        values_block,
        preferred_element_type=jnp.float32,
    )
    return (row_top, row_total, mixture)


def combine(carried, incoming):
    row_top = jnp.maximum(carried[0], incoming[0])
    old_factor = jnp.exp(carried[0] - row_top)
    new_factor = jnp.exp(incoming[0] - row_top)
    row_total = carried[1] * old_factor + incoming[1] * new_factor
    mixture = carried[2] * old_factor[..., None] + incoming[2] * new_factor[..., None]
    return (row_top, row_total, mixture)


PAGES_PER_STEP = 8


def page_attention_kernel(
    table_ref, q_ref, row_req_ref, row_pos_ref, key_req_ref, key_pos_ref,
    suffix_keys_ref, suffix_values_ref, *rest,
):
    slot_refs = rest[:PAGES_PER_STEP]
    out_ref = rest[PAGES_PER_STEP]
    scores_buf, values_buf = rest[PAGES_PER_STEP + 1 :]
    step = pl.program_id(1)
    last = pl.num_programs(1) - 1
    contract_last = (((1,), (1,)), ((), ()))

    @pl.when(step < last)
    def _():
        q = q_ref[0]
        for i in range(PAGES_PER_STEP):
            page = slot_refs[i][0]
            at = pl.multiple_of((step * PAGES_PER_STEP + i) * PAGE_TOKENS, PAGE_TOKENS)
            scores_buf[:, pl.ds(at, PAGE_TOKENS)] = lax.dot_general(
                q, page[:, :HEAD_SIZE], contract_last, preferred_element_type=jnp.float32
            )
            values_buf[pl.ds(at, PAGE_TOKENS), :] = page[:, HEAD_SIZE:]

    @pl.when(step == last)
    def _():
        rows = q_ref.shape[1]
        chunk = 128
        for r in range(0, rows, chunk):
            q = q_ref[0, r : r + chunk, :]
            mask = (row_req_ref[0, r : r + chunk, :] == key_req_ref[...]) & (
                key_pos_ref[...] <= row_pos_ref[0, r : r + chunk, :]
            )
            suffix_scores = lax.dot_general(
                q, suffix_keys_ref[...], contract_last, preferred_element_type=jnp.float32
            )
            suffix_scores = jnp.where(mask, suffix_scores, masked_low)
            prefix_scores = scores_buf[r : r + chunk, :]
            row_top = jnp.maximum(
                jnp.max(prefix_scores, axis=1, keepdims=True),
                jnp.max(suffix_scores, axis=1, keepdims=True),
            )
            prefix_weights = jnp.exp(prefix_scores - row_top)
            suffix_weights = jnp.where(mask, jnp.exp(suffix_scores - row_top), 0.0)
            row_total = jnp.sum(prefix_weights, axis=1, keepdims=True) + jnp.sum(
                suffix_weights, axis=1, keepdims=True
            )
            mixture = jnp.dot(
                prefix_weights.astype(jnp.bfloat16), values_buf[...],
                preferred_element_type=jnp.float32,
            ) + jnp.dot(
                suffix_weights.astype(jnp.bfloat16), suffix_values_ref[...],
                preferred_element_type=jnp.float32,
            )
            out_ref[0, r : r + chunk, :] = (mixture / row_total).astype(out_ref.dtype)


def page_attention(table, q, row_req, row_pos, key_req, key_pos, suffix_keys, suffix_values, slot_pages):
    pages, rows, _ = q.shape
    steps = PREFIX_PAGES // PAGES_PER_STEP
    suffix_rows = suffix_keys.shape[0]

    def slot_spec(i):
        return pl.BlockSpec(
            (1, PAGE_TOKENS, 2 * HEAD_SIZE),
            lambda p, j, t, i=i: (t[p, jnp.minimum(j * PAGES_PER_STEP + i, PREFIX_PAGES - 1)], 0, 0),
        )

    grid_spec = pltpu.PrefetchScalarGridSpec(
        num_scalar_prefetch=1,
        grid=(pages, steps + 1),
        in_specs=[
            pl.BlockSpec((1, rows, HEAD_SIZE), lambda p, j, t: (p, 0, 0)),
            pl.BlockSpec((1, rows, 1), lambda p, j, t: (p, 0, 0)),
            pl.BlockSpec((1, rows, 1), lambda p, j, t: (p, 0, 0)),
            pl.BlockSpec((1, suffix_rows), lambda p, j, t: (0, 0)),
            pl.BlockSpec((1, suffix_rows), lambda p, j, t: (0, 0)),
            pl.BlockSpec((suffix_rows, HEAD_SIZE), lambda p, j, t: (0, 0)),
            pl.BlockSpec((suffix_rows, HEAD_SIZE), lambda p, j, t: (0, 0)),
        ]
        + [slot_spec(i) for i in range(PAGES_PER_STEP)],
        out_specs=pl.BlockSpec((1, rows, HEAD_SIZE), lambda p, j, t: (p, 0, 0)),
        scratch_shapes=[
            pltpu.VMEM((rows, PREFIX_PAGES * PAGE_TOKENS), jnp.float32),
            pltpu.VMEM((PREFIX_PAGES * PAGE_TOKENS, HEAD_SIZE), jnp.bfloat16),
        ],
    )
    keys_total = PREFIX_PAGES * PAGE_TOKENS + suffix_rows
    flops = pages * rows * keys_total * HEAD_SIZE * 4
    bytes_accessed = pages * (PREFIX_PAGES * PAGE_TOKENS * 2 * HEAD_SIZE * 2 + rows * HEAD_SIZE * 4)
    return pl.pallas_call(
        page_attention_kernel,
        grid_spec=grid_spec,
        out_shape=jax.ShapeDtypeStruct((pages, rows, HEAD_SIZE), jnp.bfloat16),
        compiler_params=pltpu.CompilerParams(
            dimension_semantics=("arbitrary", "arbitrary"), vmem_limit_bytes=48 * 1024 * 1024
        ),
        cost_estimate=pl.CostEstimate(
            flops=flops, transcendentals=pages * rows * keys_total, bytes_accessed=bytes_accessed
        ),
    )(table, q, row_req, row_pos, key_req, key_pos, suffix_keys, suffix_values, *([slot_pages] * PAGES_PER_STEP))


def local(
    tokens,
    in_gain,
    w_query,
    key_projection_weight,
    value_projection_weight,
    q_gain,
    k_gain,
    w_out,
    post_gain,
    laurel_left,
    laurel_right,
    laurel_gain,
    prefix_key_slots,
    prefix_value_slots,
    prefix_slot_map,
    page_lengths,
    request_group,
    suffix_page_map,
):
    tok_count = tokens.shape[0]
    pages_here = tok_count // PAGE_TOKENS
    device = lax.axis_index("page")
    first_index = device * tok_count
    prefix_both = jnp.concatenate([prefix_key_slots, prefix_value_slots], axis=1)
    every_slot = lax.all_gather(prefix_both, "page", axis=0, tiled=True)
    requests, position, groups = token_places(first_index, tok_count, page_lengths, request_group)
    normed, queries, fresh_key_rows, fresh_value_rows = project(
        tokens,
        in_gain,
        w_query,
        key_projection_weight,
        value_projection_weight,
        q_gain,
        k_gain,
        position + PREFIX_TOKENS,
    )
    local_slot = suffix_page_map - device * pages_here
    placing = (local_slot[:, None] == jnp.arange(pages_here, dtype=jnp.int32)[None, :]).astype(
        jnp.bfloat16
    )
    both_pages = jnp.concatenate(
        [
            fresh_key_rows.reshape(pages_here, PAGE_TOKENS * HEAD_SIZE),
            fresh_value_rows.reshape(pages_here, PAGE_TOKENS * HEAD_SIZE),
        ],
        axis=1,
    )
    placed = jnp.dot(placing.T, both_pages, preferred_element_type=jnp.float32).astype(jnp.bfloat16)
    suffix_key_cache = placed[:, : PAGE_TOKENS * HEAD_SIZE].reshape(tok_count, HEAD_SIZE)
    suffix_value_cache = placed[:, PAGE_TOKENS * HEAD_SIZE :].reshape(tok_count, HEAD_SIZE)

    reach = (MAXP + pages_here - 2) // pages_here
    fresh_both = jnp.concatenate([fresh_key_rows, fresh_value_rows], axis=1)
    window = fresh_both
    covered = 1
    while covered < reach + 1:
        step = min(covered, reach + 1 - covered)
        moved = passed_along(window[: step * tok_count], "page", covered)
        window = jnp.concatenate([window, moved], axis=0)
        covered += step
    window_requests = []
    window_positions = []
    for shift_step in range(reach + 1):
        far_requests, far_position, _ = token_places(
            first_index - shift_step * tok_count, tok_count, page_lengths, request_group
        )
        window_requests.append(far_requests)
        window_positions.append(far_position)
    key_requests = jnp.concatenate(window_requests, axis=0)
    key_positions = jnp.concatenate(window_positions, axis=0)
    suffix_keys = window[:, :HEAD_SIZE]
    suffix_values = window[:, HEAD_SIZE:]

    heads = queries.shape[1]
    page_queries = queries.reshape(pages_here, PAGE_TOKENS, heads, HEAD_SIZE)
    page_requests = requests.reshape(pages_here, PAGE_TOKENS)
    page_positions = position.reshape(pages_here, PAGE_TOKENS)
    page_groups = groups.reshape(pages_here, PAGE_TOKENS)[:, 0]
    chosen = jnp.take(
        prefix_slot_map.reshape(PREFIX_COUNT, PREFIX_PAGES), page_groups, axis=0
    )
    slot_pages = every_slot.reshape(-1, PAGE_TOKENS, 2 * HEAD_SIZE)
    heads_rows = PAGE_TOKENS * heads
    attended = page_attention(
        chosen,
        page_queries.reshape(pages_here, heads_rows, HEAD_SIZE),
        jnp.repeat(page_requests, heads, axis=1)[..., None],
        jnp.repeat(page_positions, heads, axis=1)[..., None],
        key_requests[None, :],
        key_positions[None, :],
        suffix_keys,
        suffix_values,
        slot_pages,
    ).reshape(tok_count, -1)
    attn_part = jnp.dot(attended, w_out, preferred_element_type=jnp.float32)
    kv_index = lax.axis_index("kv")
    model_width = tokens.shape[1]
    half_width = model_width // lax.axis_size("kv")

    def columns(source):
        return lax.dynamic_slice_in_dim(source, kv_index * half_width, half_width, source.ndim - 1)

    partner_part = lax.ppermute(attn_part.astype(jnp.bfloat16), "kv", [(0, 1), (1, 0)])
    summed_out = attn_part + partner_part.astype(jnp.float32)
    low_rank = jnp.dot(normed, laurel_left, preferred_element_type=jnp.float32).astype(jnp.bfloat16)
    laurel_full = jnp.dot(low_rank, laurel_right, preferred_element_type=jnp.float32)
    attn_half = columns(summed_out)
    attn_branch = attn_half * rms_scale(summed_out) * columns(post_gain)
    laurel = columns(normed).astype(jnp.float32) + columns(laurel_full) * rms_scale(
        laurel_full
    ) * columns(laurel_gain)
    layer_out = (
        (columns(tokens).astype(jnp.float32) + attn_branch + laurel) * 2.0 ** (-0.5)
    ).astype(jnp.bfloat16)
    return (layer_out, suffix_key_cache, suffix_value_cache)


def solution(mesh):
    placed = (
        P("page", None),
        P(),
        P(None, "kv"),
        P(None, "kv"),
        P(None, "kv"),
        P(),
        P(),
        P("kv", None),
        P(),
        P(),
        P(),
        P(),
        P("page", "kv"),
        P("page", "kv"),
        P(),
        P(),
        P(),
        P("page"),
    )
    return jax.shard_map(
        local,
        mesh=mesh,
        in_specs=placed,
        out_specs=(P("page", "kv"), P("page", "kv"), P("page", "kv")),
        check_vma=False,
    )
```

```python
import jax
import jax.numpy as jnp
from jax import lax
from jax.sharding import PartitionSpec as P
from jax.experimental import pallas as pl
from jax.experimental.pallas import tpu as pltpu

HEAD_SIZE = 256
PAGE_TOKENS = 128
PREFIX_TOKENS = 4096
PREFIX_COUNT = 4
MAXP = 8
PREFIX_PAGES = 32


epsilon = 1e-06
rope_base = 1000000.0
masked_low = -1e30


def passed_along(block, axis, distance):
    devices = range(lax.axis_size(axis))
    route = [(i - distance, i) for i in devices if i - distance in devices]
    return lax.ppermute(block, axis, route)


def rms_scale(values):
    return lax.rsqrt(jnp.mean(values * values, axis=-1, keepdims=True) + epsilon)


def rotate(values, positions):
    half_dim = values.shape[-1] // 2
    inv_freq = rope_base ** (-(jnp.arange(half_dim).astype(jnp.float32) * 2.0 / values.shape[-1]))
    angles = positions.astype(jnp.float32)[:, None] * inv_freq[None, :]
    cosine = jnp.cos(angles)[:, None, :]
    sines = jnp.sin(angles)[:, None, :]
    first_half = values[..., :half_dim]
    second_half = values[..., half_dim:]
    return jnp.concatenate(
        [first_half * cosine - second_half * sines, second_half * cosine + first_half * sines],
        axis=-1,
    )


def project(
    tokens,
    in_gain,
    w_query,
    key_projection_weight,
    value_projection_weight,
    q_gain,
    k_gain,
    positions,
):
    tok_count = tokens.shape[0]
    tokens_wide = tokens.astype(jnp.float32)
    normed = (tokens_wide * rms_scale(tokens_wide) * in_gain).astype(jnp.bfloat16)
    queries = jnp.dot(normed, w_query, preferred_element_type=jnp.float32).reshape(
        tok_count, -1, HEAD_SIZE
    )
    queries = rotate(queries * rms_scale(queries) * q_gain, positions).astype(jnp.bfloat16)
    fresh_key_rows = jnp.dot(
        normed, key_projection_weight, preferred_element_type=jnp.float32
    ).reshape(tok_count, -1, HEAD_SIZE)
    fresh_key_rows = rotate(fresh_key_rows * rms_scale(fresh_key_rows) * k_gain, positions).astype(
        jnp.bfloat16
    )
    fresh_value_rows = jnp.dot(
        normed, value_projection_weight, preferred_element_type=jnp.float32
    ).reshape(tok_count, -1, HEAD_SIZE)
    fresh_value_rows = (fresh_value_rows * rms_scale(fresh_value_rows)).astype(jnp.bfloat16)
    return (
        normed,
        queries,
        fresh_key_rows.reshape(tok_count, HEAD_SIZE),
        fresh_value_rows.reshape(tok_count, HEAD_SIZE),
    )


def token_places(first_index, tok_count, page_lengths, request_group):
    tok_ids = first_index + jnp.arange(tok_count, dtype=jnp.int32)
    page_of = tok_ids // PAGE_TOKENS
    page_starts = jnp.cumsum(page_lengths) - page_lengths
    belongs = (page_of[:, None] >= page_starts[None, :]) & (
        page_of[:, None] < (page_starts + page_lengths)[None, :]
    )
    belongs = (belongs & (tok_ids[:, None] >= 0)).astype(jnp.int32)
    request_ids = jnp.arange(page_starts.shape[0], dtype=jnp.int32)
    requests = jnp.sum(belongs * request_ids[None, :], axis=1) - (1 - jnp.sum(belongs, axis=1))
    position = tok_ids - jnp.sum(belongs * page_starts[None, :], axis=1) * PAGE_TOKENS
    groups = jnp.sum(belongs * request_group[None, :], axis=1)
    return (requests, position, groups)


def attend(queries, keys_block, values_block, key_mask):
    scores = jnp.einsum("qhd,kd->qhk", queries, keys_block, preferred_element_type=jnp.float32)
    wide_mask = key_mask[:, None, :]
    scores = jnp.where(wide_mask, scores, masked_low)
    row_top = jnp.max(scores, axis=-1)
    weights = jnp.where(wide_mask, jnp.exp(scores - row_top[..., None]), 0.0)
    row_total = jnp.sum(weights, axis=-1)
    mixture = jnp.einsum(
        "qhk,kd->qhd",
        weights.astype(jnp.bfloat16),
        values_block,
        preferred_element_type=jnp.float32,
    )
    return (row_top, row_total, mixture)


def combine(carried, incoming):
    row_top = jnp.maximum(carried[0], incoming[0])
    old_factor = jnp.exp(carried[0] - row_top)
    new_factor = jnp.exp(incoming[0] - row_top)
    row_total = carried[1] * old_factor + incoming[1] * new_factor
    mixture = carried[2] * old_factor[..., None] + incoming[2] * new_factor[..., None]
    return (row_top, row_total, mixture)


PAGES_PER_STEP = 8


def page_attention_kernel(
    table_ref, q_ref, row_req_ref, row_pos_ref, key_req_ref, key_pos_ref,
    suffix_keys_ref, suffix_values_ref, w_out_ref, *rest,
):
    slot_refs = rest[:PAGES_PER_STEP]
    out_ref, out_low_ref = rest[PAGES_PER_STEP : PAGES_PER_STEP + 2]
    scores_buf, values_buf, suffix_buf, top_buf = rest[PAGES_PER_STEP + 2 :]
    step = pl.program_id(1)
    last = pl.num_programs(1) - 1
    contract_last = (((1,), (1,)), ((), ()))

    @pl.when(step == 0)
    def _():
        mask = (row_req_ref[0] == key_req_ref[...]) & (key_pos_ref[...] <= row_pos_ref[0])
        suffix_scores = lax.dot_general(
            q_ref[0], suffix_keys_ref[...], contract_last, preferred_element_type=jnp.float32
        )
        suffix_scores = jnp.where(mask, suffix_scores, masked_low)
        suffix_buf[...] = suffix_scores
        top_buf[...] = jnp.max(suffix_scores, axis=1, keepdims=True)

    @pl.when(step < last)
    def _():
        q = q_ref[0]
        top = top_buf[...]
        for i in range(PAGES_PER_STEP):
            page = slot_refs[i][0]
            at = pl.multiple_of((step * PAGES_PER_STEP + i) * PAGE_TOKENS, PAGE_TOKENS)
            scores = lax.dot_general(
                q, page[:, :HEAD_SIZE], contract_last, preferred_element_type=jnp.float32
            )
            scores_buf[:, pl.ds(at, PAGE_TOKENS)] = scores
            values_buf[pl.ds(at, PAGE_TOKENS), :] = page[:, HEAD_SIZE:]
            top = jnp.maximum(top, jnp.max(scores, axis=1, keepdims=True))
        top_buf[...] = top

    @pl.when(step == last)
    def _():
        rows = q_ref.shape[1]
        heads = rows // PAGE_TOKENS
        total_out = None
        for h in range(heads):
            r = h * PAGE_TOKENS
            row_top = top_buf[r : r + PAGE_TOKENS, :]
            prefix_weights = jnp.exp(scores_buf[r : r + PAGE_TOKENS, :] - row_top)
            suffix_weights = jnp.exp(suffix_buf[r : r + PAGE_TOKENS, :] - row_top)
            row_total = jnp.sum(prefix_weights, axis=1, keepdims=True) + jnp.sum(
                suffix_weights, axis=1, keepdims=True
            )
            mixture = jnp.dot(
                prefix_weights.astype(jnp.bfloat16), values_buf[...],
                preferred_element_type=jnp.float32,
            ) + jnp.dot(
                suffix_weights.astype(jnp.bfloat16), suffix_values_ref[...],
                preferred_element_type=jnp.float32,
            )
            attended = (mixture / row_total).astype(jnp.bfloat16)
            part = jnp.dot(
                attended, w_out_ref[r * 2 : r * 2 + HEAD_SIZE, :], preferred_element_type=jnp.float32
            )
            total_out = part if total_out is None else total_out + part
        out_ref[0] = total_out
        out_low_ref[0] = total_out.astype(out_low_ref.dtype)


def page_attention(table, q, row_req, row_pos, key_req, key_pos, suffix_keys, suffix_values, w_out, slot_pages):
    pages, rows, _ = q.shape
    steps = PREFIX_PAGES // PAGES_PER_STEP
    suffix_rows = suffix_keys.shape[0]
    width = w_out.shape[1]

    def slot_spec(i):
        return pl.BlockSpec(
            (1, PAGE_TOKENS, 2 * HEAD_SIZE),
            lambda p, j, t, i=i: (t[p, jnp.minimum(j * PAGES_PER_STEP + i, PREFIX_PAGES - 1)], 0, 0),
        )

    grid_spec = pltpu.PrefetchScalarGridSpec(
        num_scalar_prefetch=1,
        grid=(pages, steps + 1),
        in_specs=[
            pl.BlockSpec((1, rows, HEAD_SIZE), lambda p, j, t: (p, 0, 0)),
            pl.BlockSpec((1, rows, 1), lambda p, j, t: (p, 0, 0)),
            pl.BlockSpec((1, rows, 1), lambda p, j, t: (p, 0, 0)),
            pl.BlockSpec((1, suffix_rows), lambda p, j, t: (0, 0)),
            pl.BlockSpec((1, suffix_rows), lambda p, j, t: (0, 0)),
            pl.BlockSpec((suffix_rows, HEAD_SIZE), lambda p, j, t: (0, 0)),
            pl.BlockSpec((suffix_rows, HEAD_SIZE), lambda p, j, t: (0, 0)),
            pl.BlockSpec(w_out.shape, lambda p, j, t: (0, 0)),
        ]
        + [slot_spec(i) for i in range(PAGES_PER_STEP)],
        out_specs=[
            pl.BlockSpec((1, PAGE_TOKENS, width), lambda p, j, t: (p, 0, 0)),
            pl.BlockSpec((1, PAGE_TOKENS, width), lambda p, j, t: (p, 0, 0)),
        ],
        scratch_shapes=[
            pltpu.VMEM((rows, PREFIX_PAGES * PAGE_TOKENS), jnp.float32),
            pltpu.VMEM((PREFIX_PAGES * PAGE_TOKENS, HEAD_SIZE), jnp.bfloat16),
            pltpu.VMEM((rows, suffix_rows), jnp.float32),
            pltpu.VMEM((rows, 1), jnp.float32),
        ],
    )
    keys_total = PREFIX_PAGES * PAGE_TOKENS + suffix_rows
    flops = pages * rows * keys_total * HEAD_SIZE * 4 + pages * rows * HEAD_SIZE * width * 2
    bytes_accessed = pages * (PREFIX_PAGES * PAGE_TOKENS * 2 * HEAD_SIZE * 2 + rows * HEAD_SIZE * 2 + PAGE_TOKENS * width * 6) + w_out.size * 2
    return pl.pallas_call(
        page_attention_kernel,
        grid_spec=grid_spec,
        out_shape=(
            jax.ShapeDtypeStruct((pages, PAGE_TOKENS, width), jnp.float32),
            jax.ShapeDtypeStruct((pages, PAGE_TOKENS, width), jnp.bfloat16),
        ),
        compiler_params=pltpu.CompilerParams(
            dimension_semantics=("arbitrary", "arbitrary"), vmem_limit_bytes=56 * 1024 * 1024
        ),
        cost_estimate=pl.CostEstimate(
            flops=flops, transcendentals=pages * rows * keys_total, bytes_accessed=bytes_accessed
        ),
    )(table, q, row_req, row_pos, key_req, key_pos, suffix_keys, suffix_values, w_out, *([slot_pages] * PAGES_PER_STEP))


def local(
    tokens,
    in_gain,
    w_query,
    key_projection_weight,
    value_projection_weight,
    q_gain,
    k_gain,
    w_out,
    post_gain,
    laurel_left,
    laurel_right,
    laurel_gain,
    prefix_key_slots,
    prefix_value_slots,
    prefix_slot_map,
    page_lengths,
    request_group,
    suffix_page_map,
):
    tok_count = tokens.shape[0]
    pages_here = tok_count // PAGE_TOKENS
    device = lax.axis_index("page")
    first_index = device * tok_count
    prefix_both = jnp.concatenate([prefix_key_slots, prefix_value_slots], axis=1)
    every_slot = lax.all_gather(prefix_both, "page", axis=0, tiled=True)
    requests, position, groups = token_places(first_index, tok_count, page_lengths, request_group)
    normed, queries, fresh_key_rows, fresh_value_rows = project(
        tokens,
        in_gain,
        w_query,
        key_projection_weight,
        value_projection_weight,
        q_gain,
        k_gain,
        position + PREFIX_TOKENS,
    )
    local_slot = suffix_page_map - device * pages_here
    placing = (local_slot[:, None] == jnp.arange(pages_here, dtype=jnp.int32)[None, :]).astype(
        jnp.bfloat16
    )
    both_pages = jnp.concatenate(
        [
            fresh_key_rows.reshape(pages_here, PAGE_TOKENS * HEAD_SIZE),
            fresh_value_rows.reshape(pages_here, PAGE_TOKENS * HEAD_SIZE),
        ],
        axis=1,
    )
    placed = jnp.dot(placing.T, both_pages, preferred_element_type=jnp.float32).astype(jnp.bfloat16)
    suffix_key_cache = placed[:, : PAGE_TOKENS * HEAD_SIZE].reshape(tok_count, HEAD_SIZE)
    suffix_value_cache = placed[:, PAGE_TOKENS * HEAD_SIZE :].reshape(tok_count, HEAD_SIZE)

    reach = (MAXP + pages_here - 2) // pages_here
    fresh_both = jnp.concatenate([fresh_key_rows, fresh_value_rows], axis=1)
    window = fresh_both
    covered = 1
    while covered < reach + 1:
        step = min(covered, reach + 1 - covered)
        moved = passed_along(window[: step * tok_count], "page", covered)
        window = jnp.concatenate([window, moved], axis=0)
        covered += step
    window_requests = []
    window_positions = []
    for shift_step in range(reach + 1):
        far_requests, far_position, _ = token_places(
            first_index - shift_step * tok_count, tok_count, page_lengths, request_group
        )
        window_requests.append(far_requests)
        window_positions.append(far_position)
    key_requests = jnp.concatenate(window_requests, axis=0)
    key_positions = jnp.concatenate(window_positions, axis=0)
    suffix_keys = window[:, :HEAD_SIZE]
    suffix_values = window[:, HEAD_SIZE:]

    heads = queries.shape[1]
    page_queries = queries.reshape(pages_here, PAGE_TOKENS, heads, HEAD_SIZE)
    page_requests = requests.reshape(pages_here, PAGE_TOKENS)
    page_positions = position.reshape(pages_here, PAGE_TOKENS)
    page_groups = groups.reshape(pages_here, PAGE_TOKENS)[:, 0]
    chosen = jnp.take(
        prefix_slot_map.reshape(PREFIX_COUNT, PREFIX_PAGES), page_groups, axis=0
    )
    slot_pages = every_slot.reshape(-1, PAGE_TOKENS, 2 * HEAD_SIZE)
    heads_rows = PAGE_TOKENS * heads
    kv_index = lax.axis_index("kv")
    model_width = tokens.shape[1]
    half_width = model_width // lax.axis_size("kv")

    def columns(source):
        return lax.dynamic_slice_in_dim(source, kv_index * half_width, half_width, source.ndim - 1)

    low_rank = jnp.dot(normed, laurel_left, preferred_element_type=jnp.float32).astype(jnp.bfloat16)
    laurel_full = jnp.dot(low_rank, laurel_right, preferred_element_type=jnp.float32)
    laurel = columns(normed).astype(jnp.float32) + columns(laurel_full) * rms_scale(
        laurel_full
    ) * columns(laurel_gain)
    resident = columns(tokens).astype(jnp.float32) + laurel
    head_queries = jnp.swapaxes(page_queries, 1, 2).reshape(pages_here, heads_rows, HEAD_SIZE)
    row_requests = jnp.tile(page_requests, (1, heads))[..., None]
    row_positions = jnp.tile(page_positions, (1, heads))[..., None]
    (
        resident,
        suffix_key_cache,
        suffix_value_cache,
        head_queries,
        row_requests,
        row_positions,
        suffix_keys,
        suffix_values,
    ) = lax.optimization_barrier(
        (
            resident,
            suffix_key_cache,
            suffix_value_cache,
            head_queries,
            row_requests,
            row_positions,
            suffix_keys,
            suffix_values,
        )
    )
    attn_part, attn_low = page_attention(
        chosen,
        head_queries,
        row_requests,
        row_positions,
        key_requests[None, :],
        key_positions[None, :],
        suffix_keys,
        suffix_values,
        w_out,
        slot_pages,
    )
    attn_part = attn_part.reshape(tok_count, model_width)
    partner_part = lax.ppermute(attn_low.reshape(tok_count, model_width), "kv", [(0, 1), (1, 0)])
    summed_out = attn_part + partner_part.astype(jnp.float32)
    attn_branch = columns(summed_out) * rms_scale(summed_out) * columns(post_gain)
    layer_out = ((resident + attn_branch) * 2.0 ** (-0.5)).astype(jnp.bfloat16)
    return (layer_out, suffix_key_cache, suffix_value_cache)


def solution(mesh):
    placed = (
        P("page", None),
        P(),
        P(None, "kv"),
        P(None, "kv"),
        P(None, "kv"),
        P(),
        P(),
        P("kv", None),
        P(),
        P(),
        P(),
        P(),
        P("page", "kv"),
        P("page", "kv"),
        P(),
        P(),
        P(),
        P("page"),
    )
    return jax.shard_map(
        local,
        mesh=mesh,
        in_specs=placed,
        out_specs=(P("page", "kv"), P("page", "kv"), P("page", "kv")),
        check_vma=False,
    )
```

```python
import jax
import jax.numpy as jnp
from jax import lax
from jax.sharding import PartitionSpec as P
from jax.experimental import pallas as pl
from jax.experimental.pallas import tpu as pltpu

HEAD_SIZE = 256
PAGE_TOKENS = 128
PREFIX_TOKENS = 4096
PREFIX_COUNT = 4
MAXP = 8
PREFIX_PAGES = 32


epsilon = 1e-06
rope_base = 1000000.0
masked_low = -1e30


def passed_along(block, axis, distance):
    devices = range(lax.axis_size(axis))
    route = [(i - distance, i) for i in devices if i - distance in devices]
    return lax.ppermute(block, axis, route)


def rms_scale(values):
    return lax.rsqrt(jnp.mean(values * values, axis=-1, keepdims=True) + epsilon)


def rotate(values, positions):
    half_dim = values.shape[-1] // 2
    inv_freq = rope_base ** (-(jnp.arange(half_dim).astype(jnp.float32) * 2.0 / values.shape[-1]))
    angles = positions.astype(jnp.float32)[:, None] * inv_freq[None, :]
    cosine = jnp.cos(angles)[:, None, :]
    sines = jnp.sin(angles)[:, None, :]
    first_half = values[..., :half_dim]
    second_half = values[..., half_dim:]
    return jnp.concatenate(
        [first_half * cosine - second_half * sines, second_half * cosine + first_half * sines],
        axis=-1,
    )


def project(
    tokens,
    in_gain,
    w_query,
    key_projection_weight,
    value_projection_weight,
    q_gain,
    k_gain,
    positions,
):
    tok_count = tokens.shape[0]
    tokens_wide = tokens.astype(jnp.float32)
    normed = (tokens_wide * rms_scale(tokens_wide) * in_gain).astype(jnp.bfloat16)
    queries = jnp.dot(normed, w_query, preferred_element_type=jnp.float32).reshape(
        tok_count, -1, HEAD_SIZE
    )
    queries = rotate(queries * rms_scale(queries) * q_gain, positions).astype(jnp.bfloat16)
    fresh_key_rows = jnp.dot(
        normed, key_projection_weight, preferred_element_type=jnp.float32
    ).reshape(tok_count, -1, HEAD_SIZE)
    fresh_key_rows = rotate(fresh_key_rows * rms_scale(fresh_key_rows) * k_gain, positions).astype(
        jnp.bfloat16
    )
    fresh_value_rows = jnp.dot(
        normed, value_projection_weight, preferred_element_type=jnp.float32
    ).reshape(tok_count, -1, HEAD_SIZE)
    fresh_value_rows = (fresh_value_rows * rms_scale(fresh_value_rows)).astype(jnp.bfloat16)
    return (
        normed,
        queries,
        fresh_key_rows.reshape(tok_count, HEAD_SIZE),
        fresh_value_rows.reshape(tok_count, HEAD_SIZE),
    )


def token_places(first_index, tok_count, page_lengths, request_group):
    tok_ids = first_index + jnp.arange(tok_count, dtype=jnp.int32)
    page_of = tok_ids // PAGE_TOKENS
    page_starts = jnp.cumsum(page_lengths) - page_lengths
    belongs = (page_of[:, None] >= page_starts[None, :]) & (
        page_of[:, None] < (page_starts + page_lengths)[None, :]
    )
    belongs = (belongs & (tok_ids[:, None] >= 0)).astype(jnp.int32)
    request_ids = jnp.arange(page_starts.shape[0], dtype=jnp.int32)
    requests = jnp.sum(belongs * request_ids[None, :], axis=1) - (1 - jnp.sum(belongs, axis=1))
    position = tok_ids - jnp.sum(belongs * page_starts[None, :], axis=1) * PAGE_TOKENS
    groups = jnp.sum(belongs * request_group[None, :], axis=1)
    return (requests, position, groups)


def attend(queries, keys_block, values_block, key_mask):
    scores = jnp.einsum("qhd,kd->qhk", queries, keys_block, preferred_element_type=jnp.float32)
    wide_mask = key_mask[:, None, :]
    scores = jnp.where(wide_mask, scores, masked_low)
    row_top = jnp.max(scores, axis=-1)
    weights = jnp.where(wide_mask, jnp.exp(scores - row_top[..., None]), 0.0)
    row_total = jnp.sum(weights, axis=-1)
    mixture = jnp.einsum(
        "qhk,kd->qhd",
        weights.astype(jnp.bfloat16),
        values_block,
        preferred_element_type=jnp.float32,
    )
    return (row_top, row_total, mixture)


def combine(carried, incoming):
    row_top = jnp.maximum(carried[0], incoming[0])
    old_factor = jnp.exp(carried[0] - row_top)
    new_factor = jnp.exp(incoming[0] - row_top)
    row_total = carried[1] * old_factor + incoming[1] * new_factor
    mixture = carried[2] * old_factor[..., None] + incoming[2] * new_factor[..., None]
    return (row_top, row_total, mixture)


PAGES_PER_STEP = 8


def page_attention_kernel(
    table_ref, q_ref, row_req_ref, row_pos_ref, key_req_ref, key_pos_ref,
    suffix_keys_ref, suffix_values_ref, w_out_ref, *rest,
):
    slot_refs = rest[:PAGES_PER_STEP]
    out_ref, out_low_ref = rest[PAGES_PER_STEP : PAGES_PER_STEP + 2]
    scores_buf, keys_buf, values_buf, suffix_buf, top_buf = rest[PAGES_PER_STEP + 2 :]
    step = pl.program_id(1)
    last = pl.num_programs(1) - 1
    contract_last = (((1,), (1,)), ((), ()))

    @pl.when(step == 0)
    def _():
        mask = (row_req_ref[0] == key_req_ref[...]) & (key_pos_ref[...] <= row_pos_ref[0])
        suffix_scores = lax.dot_general(
            q_ref[0], suffix_keys_ref[...], contract_last, preferred_element_type=jnp.float32
        )
        suffix_scores = jnp.where(mask, suffix_scores, masked_low)
        suffix_buf[...] = suffix_scores
        top_buf[...] = jnp.max(suffix_scores, axis=1, keepdims=True)

    @pl.when(step < last)
    def _():
        base = pl.multiple_of(step * (PAGES_PER_STEP * PAGE_TOKENS), PAGES_PER_STEP * PAGE_TOKENS)
        for i in range(PAGES_PER_STEP):
            page = slot_refs[i][0]
            at = pl.multiple_of(base + i * PAGE_TOKENS, PAGE_TOKENS)
            keys_buf[pl.ds(at, PAGE_TOKENS), :] = page[:, :HEAD_SIZE]
            values_buf[pl.ds(at, PAGE_TOKENS), :] = page[:, HEAD_SIZE:]
        scores = lax.dot_general(
            q_ref[0], keys_buf[pl.ds(base, PAGES_PER_STEP * PAGE_TOKENS), :], contract_last,
            preferred_element_type=jnp.float32,
        )
        scores_buf[:, pl.ds(base, PAGES_PER_STEP * PAGE_TOKENS)] = scores
        top_buf[...] = jnp.maximum(top_buf[...], jnp.max(scores, axis=1, keepdims=True))

    @pl.when(step == last)
    def _():
        rows = q_ref.shape[1]
        heads = rows // PAGE_TOKENS
        chunk = 512
        chunks = PREFIX_PAGES * PAGE_TOKENS // chunk
        total_out = None
        for h in range(heads):
            r = h * PAGE_TOKENS
            row_top = top_buf[r : r + PAGE_TOKENS, :]
            suffix_weights = jnp.exp(suffix_buf[r : r + PAGE_TOKENS, :] - row_top)
            row_total = jnp.sum(suffix_weights, axis=1, keepdims=True)
            mixture = jnp.dot(
                suffix_weights.astype(jnp.bfloat16), suffix_values_ref[...],
                preferred_element_type=jnp.float32,
            )

            def one_chunk(c, carry, r=r, row_top=row_top):
                row_total, mixture = carry
                at = pl.multiple_of(c * chunk, chunk)
                weights = jnp.exp(scores_buf[r : r + PAGE_TOKENS, pl.ds(at, chunk)] - row_top)
                row_total = row_total + jnp.sum(weights, axis=1, keepdims=True)
                mixture = mixture + jnp.dot(
                    weights.astype(jnp.bfloat16), values_buf[pl.ds(at, chunk), :],
                    preferred_element_type=jnp.float32,
                )
                return row_total, mixture

            row_total, mixture = lax.fori_loop(0, chunks, one_chunk, (row_total, mixture))
            attended = (mixture / row_total).astype(jnp.bfloat16)
            part = jnp.dot(
                attended, w_out_ref[r * 2 : r * 2 + HEAD_SIZE, :], preferred_element_type=jnp.float32
            )
            total_out = part if total_out is None else total_out + part
        out_ref[0] = total_out
        out_low_ref[0] = total_out.astype(out_low_ref.dtype)


def page_attention(table, q, row_req, row_pos, key_req, key_pos, suffix_keys, suffix_values, w_out, slot_pages):
    pages, rows, _ = q.shape
    steps = PREFIX_PAGES // PAGES_PER_STEP
    suffix_rows = suffix_keys.shape[0]
    width = w_out.shape[1]

    def slot_spec(i):
        return pl.BlockSpec(
            (1, PAGE_TOKENS, 2 * HEAD_SIZE),
            lambda p, j, t, i=i: (t[p, jnp.minimum(j * PAGES_PER_STEP + i, PREFIX_PAGES - 1)], 0, 0),
        )

    grid_spec = pltpu.PrefetchScalarGridSpec(
        num_scalar_prefetch=1,
        grid=(pages, steps + 1),
        in_specs=[
            pl.BlockSpec((1, rows, HEAD_SIZE), lambda p, j, t: (p, 0, 0)),
            pl.BlockSpec((1, rows, 1), lambda p, j, t: (p, 0, 0)),
            pl.BlockSpec((1, rows, 1), lambda p, j, t: (p, 0, 0)),
            pl.BlockSpec((1, suffix_rows), lambda p, j, t: (0, 0)),
            pl.BlockSpec((1, suffix_rows), lambda p, j, t: (0, 0)),
            pl.BlockSpec((suffix_rows, HEAD_SIZE), lambda p, j, t: (0, 0)),
            pl.BlockSpec((suffix_rows, HEAD_SIZE), lambda p, j, t: (0, 0)),
            pl.BlockSpec(w_out.shape, lambda p, j, t: (0, 0)),
        ]
        + [slot_spec(i) for i in range(PAGES_PER_STEP)],
        out_specs=[
            pl.BlockSpec((1, PAGE_TOKENS, width), lambda p, j, t: (p, 0, 0)),
            pl.BlockSpec((1, PAGE_TOKENS, width), lambda p, j, t: (p, 0, 0)),
        ],
        scratch_shapes=[
            pltpu.VMEM((rows, PREFIX_PAGES * PAGE_TOKENS), jnp.float32),
            pltpu.VMEM((PREFIX_PAGES * PAGE_TOKENS, HEAD_SIZE), jnp.bfloat16),
            pltpu.VMEM((PREFIX_PAGES * PAGE_TOKENS, HEAD_SIZE), jnp.bfloat16),
            pltpu.VMEM((rows, suffix_rows), jnp.float32),
            pltpu.VMEM((rows, 1), jnp.float32),
        ],
    )
    keys_total = PREFIX_PAGES * PAGE_TOKENS + suffix_rows
    flops = pages * rows * keys_total * HEAD_SIZE * 4 + pages * rows * HEAD_SIZE * width * 2
    bytes_accessed = pages * (PREFIX_PAGES * PAGE_TOKENS * 2 * HEAD_SIZE * 2 + rows * HEAD_SIZE * 2 + PAGE_TOKENS * width * 6) + w_out.size * 2
    return pl.pallas_call(
        page_attention_kernel,
        grid_spec=grid_spec,
        out_shape=(
            jax.ShapeDtypeStruct((pages, PAGE_TOKENS, width), jnp.float32),
            jax.ShapeDtypeStruct((pages, PAGE_TOKENS, width), jnp.bfloat16),
        ),
        compiler_params=pltpu.CompilerParams(
            dimension_semantics=("arbitrary", "arbitrary"), vmem_limit_bytes=56 * 1024 * 1024
        ),
        cost_estimate=pl.CostEstimate(
            flops=flops, transcendentals=pages * rows * keys_total, bytes_accessed=bytes_accessed
        ),
    )(table, q, row_req, row_pos, key_req, key_pos, suffix_keys, suffix_values, w_out, *([slot_pages] * PAGES_PER_STEP))


def local(
    tokens,
    in_gain,
    w_query,
    key_projection_weight,
    value_projection_weight,
    q_gain,
    k_gain,
    w_out,
    post_gain,
    laurel_left,
    laurel_right,
    laurel_gain,
    prefix_key_slots,
    prefix_value_slots,
    prefix_slot_map,
    page_lengths,
    request_group,
    suffix_page_map,
):
    tok_count = tokens.shape[0]
    pages_here = tok_count // PAGE_TOKENS
    device = lax.axis_index("page")
    first_index = device * tok_count
    prefix_both = jnp.concatenate([prefix_key_slots, prefix_value_slots], axis=1)
    every_slot = lax.all_gather(prefix_both, "page", axis=0, tiled=True)
    requests, position, groups = token_places(first_index, tok_count, page_lengths, request_group)
    normed, queries, fresh_key_rows, fresh_value_rows = project(
        tokens,
        in_gain,
        w_query,
        key_projection_weight,
        value_projection_weight,
        q_gain,
        k_gain,
        position + PREFIX_TOKENS,
    )
    local_slot = suffix_page_map - device * pages_here
    placing = (local_slot[:, None] == jnp.arange(pages_here, dtype=jnp.int32)[None, :]).astype(
        jnp.bfloat16
    )
    both_pages = jnp.concatenate(
        [
            fresh_key_rows.reshape(pages_here, PAGE_TOKENS * HEAD_SIZE),
            fresh_value_rows.reshape(pages_here, PAGE_TOKENS * HEAD_SIZE),
        ],
        axis=1,
    )
    placed = jnp.dot(placing.T, both_pages, preferred_element_type=jnp.float32).astype(jnp.bfloat16)
    suffix_key_cache = placed[:, : PAGE_TOKENS * HEAD_SIZE].reshape(tok_count, HEAD_SIZE)
    suffix_value_cache = placed[:, PAGE_TOKENS * HEAD_SIZE :].reshape(tok_count, HEAD_SIZE)

    reach = (MAXP + pages_here - 2) // pages_here
    fresh_both = jnp.concatenate([fresh_key_rows, fresh_value_rows], axis=1)
    window = fresh_both
    covered = 1
    while covered < reach + 1:
        step = min(covered, reach + 1 - covered)
        moved = passed_along(window[: step * tok_count], "page", covered)
        window = jnp.concatenate([window, moved], axis=0)
        covered += step
    window_requests = []
    window_positions = []
    for shift_step in range(reach + 1):
        far_requests, far_position, _ = token_places(
            first_index - shift_step * tok_count, tok_count, page_lengths, request_group
        )
        window_requests.append(far_requests)
        window_positions.append(far_position)
    key_requests = jnp.concatenate(window_requests, axis=0)
    key_positions = jnp.concatenate(window_positions, axis=0)
    suffix_keys = window[:, :HEAD_SIZE]
    suffix_values = window[:, HEAD_SIZE:]

    heads = queries.shape[1]
    page_queries = queries.reshape(pages_here, PAGE_TOKENS, heads, HEAD_SIZE)
    page_requests = requests.reshape(pages_here, PAGE_TOKENS)
    page_positions = position.reshape(pages_here, PAGE_TOKENS)
    page_groups = groups.reshape(pages_here, PAGE_TOKENS)[:, 0]
    chosen = jnp.take(
        prefix_slot_map.reshape(PREFIX_COUNT, PREFIX_PAGES), page_groups, axis=0
    )
    slot_pages = every_slot.reshape(-1, PAGE_TOKENS, 2 * HEAD_SIZE)
    heads_rows = PAGE_TOKENS * heads
    kv_index = lax.axis_index("kv")
    model_width = tokens.shape[1]
    half_width = model_width // lax.axis_size("kv")

    def columns(source):
        return lax.dynamic_slice_in_dim(source, kv_index * half_width, half_width, source.ndim - 1)

    low_rank = jnp.dot(normed, laurel_left, preferred_element_type=jnp.float32).astype(jnp.bfloat16)
    laurel_full = jnp.dot(low_rank, laurel_right, preferred_element_type=jnp.float32)
    laurel = columns(normed).astype(jnp.float32) + columns(laurel_full) * rms_scale(
        laurel_full
    ) * columns(laurel_gain)
    resident = columns(tokens).astype(jnp.float32) + laurel
    head_queries = jnp.swapaxes(page_queries, 1, 2).reshape(pages_here, heads_rows, HEAD_SIZE)
    row_requests = jnp.tile(page_requests, (1, heads))[..., None]
    row_positions = jnp.tile(page_positions, (1, heads))[..., None]
    (
        resident,
        suffix_key_cache,
        suffix_value_cache,
        head_queries,
        row_requests,
        row_positions,
        suffix_keys,
        suffix_values,
    ) = lax.optimization_barrier(
        (
            resident,
            suffix_key_cache,
            suffix_value_cache,
            head_queries,
            row_requests,
            row_positions,
            suffix_keys,
            suffix_values,
        )
    )
    attn_part, attn_low = page_attention(
        chosen,
        head_queries,
        row_requests,
        row_positions,
        key_requests[None, :],
        key_positions[None, :],
        suffix_keys,
        suffix_values,
        w_out,
        slot_pages,
    )
    attn_part = attn_part.reshape(tok_count, model_width)
    partner_part = lax.ppermute(attn_low.reshape(tok_count, model_width), "kv", [(0, 1), (1, 0)])
    summed_out = attn_part + partner_part.astype(jnp.float32)
    attn_branch = columns(summed_out) * rms_scale(summed_out) * columns(post_gain)
    layer_out = ((resident + attn_branch) * 2.0 ** (-0.5)).astype(jnp.bfloat16)
    return (layer_out, suffix_key_cache, suffix_value_cache)


def solution(mesh):
    placed = (
        P("page", None),
        P(),
        P(None, "kv"),
        P(None, "kv"),
        P(None, "kv"),
        P(),
        P(),
        P("kv", None),
        P(),
        P(),
        P(),
        P(),
        P("page", "kv"),
        P("page", "kv"),
        P(),
        P(),
        P(),
        P("page"),
    )
    return jax.shard_map(
        local,
        mesh=mesh,
        in_specs=placed,
        out_specs=(P("page", "kv"), P("page", "kv"), P("page", "kv")),
        check_vma=False,
    )
```

```python
import jax
import jax.numpy as jnp
from jax import lax
from jax.sharding import PartitionSpec as P
from jax.experimental import pallas as pl
from jax.experimental.pallas import tpu as pltpu

HEAD_SIZE = 256
PAGE_TOKENS = 128
PREFIX_TOKENS = 4096
PREFIX_COUNT = 4
MAXP = 8
PREFIX_PAGES = 32


epsilon = 1e-06
rope_base = 1000000.0
masked_low = -1e30


def passed_along(block, axis, distance):
    devices = range(lax.axis_size(axis))
    route = [(i - distance, i) for i in devices if i - distance in devices]
    return lax.ppermute(block, axis, route)


def rms_scale(values):
    return lax.rsqrt(jnp.mean(values * values, axis=-1, keepdims=True) + epsilon)


def rotate(values, positions):
    half_dim = values.shape[-1] // 2
    inv_freq = rope_base ** (-(jnp.arange(half_dim).astype(jnp.float32) * 2.0 / values.shape[-1]))
    angles = positions.astype(jnp.float32)[:, None] * inv_freq[None, :]
    cosine = jnp.cos(angles)[:, None, :]
    sines = jnp.sin(angles)[:, None, :]
    first_half = values[..., :half_dim]
    second_half = values[..., half_dim:]
    return jnp.concatenate(
        [first_half * cosine - second_half * sines, second_half * cosine + first_half * sines],
        axis=-1,
    )


def project(
    tokens,
    in_gain,
    w_query,
    key_projection_weight,
    value_projection_weight,
    q_gain,
    k_gain,
    positions,
):
    tok_count = tokens.shape[0]
    tokens_wide = tokens.astype(jnp.float32)
    normed = (tokens_wide * rms_scale(tokens_wide) * in_gain).astype(jnp.bfloat16)
    queries = jnp.dot(normed, w_query, preferred_element_type=jnp.float32).reshape(
        tok_count, -1, HEAD_SIZE
    )
    queries = rotate(queries * rms_scale(queries) * q_gain, positions).astype(jnp.bfloat16)
    fresh_key_rows = jnp.dot(
        normed, key_projection_weight, preferred_element_type=jnp.float32
    ).reshape(tok_count, -1, HEAD_SIZE)
    fresh_key_rows = rotate(fresh_key_rows * rms_scale(fresh_key_rows) * k_gain, positions).astype(
        jnp.bfloat16
    )
    fresh_value_rows = jnp.dot(
        normed, value_projection_weight, preferred_element_type=jnp.float32
    ).reshape(tok_count, -1, HEAD_SIZE)
    fresh_value_rows = (fresh_value_rows * rms_scale(fresh_value_rows)).astype(jnp.bfloat16)
    return (
        normed,
        queries,
        fresh_key_rows.reshape(tok_count, HEAD_SIZE),
        fresh_value_rows.reshape(tok_count, HEAD_SIZE),
    )


def token_places(first_index, tok_count, page_lengths, request_group):
    tok_ids = first_index + jnp.arange(tok_count, dtype=jnp.int32)
    page_of = tok_ids // PAGE_TOKENS
    page_starts = jnp.cumsum(page_lengths) - page_lengths
    belongs = (page_of[:, None] >= page_starts[None, :]) & (
        page_of[:, None] < (page_starts + page_lengths)[None, :]
    )
    belongs = (belongs & (tok_ids[:, None] >= 0)).astype(jnp.int32)
    request_ids = jnp.arange(page_starts.shape[0], dtype=jnp.int32)
    requests = jnp.sum(belongs * request_ids[None, :], axis=1) - (1 - jnp.sum(belongs, axis=1))
    position = tok_ids - jnp.sum(belongs * page_starts[None, :], axis=1) * PAGE_TOKENS
    groups = jnp.sum(belongs * request_group[None, :], axis=1)
    return (requests, position, groups)


def attend(queries, keys_block, values_block, key_mask):
    scores = jnp.einsum("qhd,kd->qhk", queries, keys_block, preferred_element_type=jnp.float32)
    wide_mask = key_mask[:, None, :]
    scores = jnp.where(wide_mask, scores, masked_low)
    row_top = jnp.max(scores, axis=-1)
    weights = jnp.where(wide_mask, jnp.exp(scores - row_top[..., None]), 0.0)
    row_total = jnp.sum(weights, axis=-1)
    mixture = jnp.einsum(
        "qhk,kd->qhd",
        weights.astype(jnp.bfloat16),
        values_block,
        preferred_element_type=jnp.float32,
    )
    return (row_top, row_total, mixture)


def combine(carried, incoming):
    row_top = jnp.maximum(carried[0], incoming[0])
    old_factor = jnp.exp(carried[0] - row_top)
    new_factor = jnp.exp(incoming[0] - row_top)
    row_total = carried[1] * old_factor + incoming[1] * new_factor
    mixture = carried[2] * old_factor[..., None] + incoming[2] * new_factor[..., None]
    return (row_top, row_total, mixture)


PAGES_PER_STEP = 8


def page_attention_kernel(
    table_ref, q_ref, row_req_ref, row_pos_ref, key_req_ref, key_pos_ref,
    suffix_keys_ref, suffix_values_ref, w_out_ref, *rest,
):
    slot_refs = rest[:PAGES_PER_STEP]
    out_ref, out_low_ref = rest[PAGES_PER_STEP : PAGES_PER_STEP + 2]
    scores_buf, values_buf, suffix_buf, top_buf = rest[PAGES_PER_STEP + 2 :]
    step = pl.program_id(1)
    last = pl.num_programs(1) - 1
    contract_last = (((1,), (1,)), ((), ()))

    @pl.when(step == 0)
    def _():
        mask = (row_req_ref[0] == key_req_ref[...]) & (key_pos_ref[...] <= row_pos_ref[0])
        suffix_scores = lax.dot_general(
            q_ref[0], suffix_keys_ref[...], contract_last, preferred_element_type=jnp.float32
        )
        suffix_scores = jnp.where(mask, suffix_scores, masked_low)
        suffix_buf[...] = suffix_scores
        top_buf[...] = jnp.max(suffix_scores, axis=1, keepdims=True)

    @pl.when(step < last)
    def _():
        q = q_ref[0]
        top = top_buf[...]
        for i in range(PAGES_PER_STEP):
            page = slot_refs[i][0]
            at = pl.multiple_of((step * PAGES_PER_STEP + i) * PAGE_TOKENS, PAGE_TOKENS)
            scores = lax.dot_general(
                q, page[:, :HEAD_SIZE], contract_last, preferred_element_type=jnp.float32
            )
            scores_buf[:, pl.ds(at, PAGE_TOKENS)] = scores
            values_buf[pl.ds(at, PAGE_TOKENS), :] = page[:, HEAD_SIZE:]
            top = jnp.maximum(top, jnp.max(scores, axis=1, keepdims=True))
        top_buf[...] = top

    @pl.when(step == last)
    def _():
        rows = q_ref.shape[1]
        heads = rows // PAGE_TOKENS
        total_out = None
        for h in range(heads):
            r = h * PAGE_TOKENS
            row_top = top_buf[r : r + PAGE_TOKENS, :]
            prefix_weights = jnp.exp(scores_buf[r : r + PAGE_TOKENS, :] - row_top)
            suffix_weights = jnp.exp(suffix_buf[r : r + PAGE_TOKENS, :] - row_top)
            row_total = jnp.sum(prefix_weights, axis=1, keepdims=True) + jnp.sum(
                suffix_weights, axis=1, keepdims=True
            )
            mixture = jnp.dot(
                prefix_weights.astype(jnp.bfloat16), values_buf[...],
                preferred_element_type=jnp.float32,
            ) + jnp.dot(
                suffix_weights.astype(jnp.bfloat16), suffix_values_ref[...],
                preferred_element_type=jnp.float32,
            )
            attended = (mixture / row_total).astype(jnp.bfloat16)
            part = jnp.dot(
                attended, w_out_ref[r * 2 : r * 2 + HEAD_SIZE, :], preferred_element_type=jnp.float32
            )
            total_out = part if total_out is None else total_out + part
        out_ref[0] = total_out
        out_low_ref[0] = total_out.astype(out_low_ref.dtype)


def page_attention(table, q, row_req, row_pos, key_req, key_pos, suffix_keys, suffix_values, w_out, slot_pages):
    pages, rows, _ = q.shape
    steps = PREFIX_PAGES // PAGES_PER_STEP
    suffix_rows = suffix_keys.shape[0]
    width = w_out.shape[1]

    def slot_spec(i):
        return pl.BlockSpec(
            (1, PAGE_TOKENS, 2 * HEAD_SIZE),
            lambda p, j, t, i=i: (t[p, jnp.minimum(j * PAGES_PER_STEP + i, PREFIX_PAGES - 1)], 0, 0),
        )

    grid_spec = pltpu.PrefetchScalarGridSpec(
        num_scalar_prefetch=1,
        grid=(pages, steps + 1),
        in_specs=[
            pl.BlockSpec((1, rows, HEAD_SIZE), lambda p, j, t: (p, 0, 0)),
            pl.BlockSpec((1, rows, 1), lambda p, j, t: (p, 0, 0)),
            pl.BlockSpec((1, rows, 1), lambda p, j, t: (p, 0, 0)),
            pl.BlockSpec((1, suffix_rows), lambda p, j, t: (0, 0)),
            pl.BlockSpec((1, suffix_rows), lambda p, j, t: (0, 0)),
            pl.BlockSpec((suffix_rows, HEAD_SIZE), lambda p, j, t: (0, 0)),
            pl.BlockSpec((suffix_rows, HEAD_SIZE), lambda p, j, t: (0, 0)),
            pl.BlockSpec(w_out.shape, lambda p, j, t: (0, 0)),
        ]
        + [slot_spec(i) for i in range(PAGES_PER_STEP)],
        out_specs=[
            pl.BlockSpec((1, PAGE_TOKENS, width), lambda p, j, t: (p, 0, 0)),
            pl.BlockSpec((1, PAGE_TOKENS, width), lambda p, j, t: (p, 0, 0)),
        ],
        scratch_shapes=[
            pltpu.VMEM((rows, PREFIX_PAGES * PAGE_TOKENS), jnp.float32),
            pltpu.VMEM((PREFIX_PAGES * PAGE_TOKENS, HEAD_SIZE), jnp.bfloat16),
            pltpu.VMEM((rows, suffix_rows), jnp.float32),
            pltpu.VMEM((rows, 1), jnp.float32),
        ],
    )
    keys_total = PREFIX_PAGES * PAGE_TOKENS + suffix_rows
    flops = pages * rows * keys_total * HEAD_SIZE * 4 + pages * rows * HEAD_SIZE * width * 2
    bytes_accessed = pages * (PREFIX_PAGES * PAGE_TOKENS * 2 * HEAD_SIZE * 2 + rows * HEAD_SIZE * 2 + PAGE_TOKENS * width * 6) + w_out.size * 2
    return pl.pallas_call(
        page_attention_kernel,
        grid_spec=grid_spec,
        out_shape=(
            jax.ShapeDtypeStruct((pages, PAGE_TOKENS, width), jnp.float32),
            jax.ShapeDtypeStruct((pages, PAGE_TOKENS, width), jnp.bfloat16),
        ),
        compiler_params=pltpu.CompilerParams(
            dimension_semantics=("arbitrary", "arbitrary"), vmem_limit_bytes=56 * 1024 * 1024
        ),
        cost_estimate=pl.CostEstimate(
            flops=flops, transcendentals=pages * rows * keys_total, bytes_accessed=bytes_accessed
        ),
    )(table, q, row_req, row_pos, key_req, key_pos, suffix_keys, suffix_values, w_out, *([slot_pages] * PAGES_PER_STEP))


def local(
    tokens,
    in_gain,
    w_query,
    key_projection_weight,
    value_projection_weight,
    q_gain,
    k_gain,
    w_out,
    post_gain,
    laurel_left,
    laurel_right,
    laurel_gain,
    prefix_key_slots,
    prefix_value_slots,
    prefix_slot_map,
    page_lengths,
    request_group,
    suffix_page_map,
):
    tok_count = tokens.shape[0]
    pages_here = tok_count // PAGE_TOKENS
    device = lax.axis_index("page")
    first_index = device * tok_count
    prefix_both = jnp.concatenate([prefix_key_slots, prefix_value_slots], axis=1)
    every_slot = lax.all_gather(prefix_both, "page", axis=0, tiled=True)
    requests, position, groups = token_places(first_index, tok_count, page_lengths, request_group)
    normed, queries, fresh_key_rows, fresh_value_rows = project(
        tokens,
        in_gain,
        w_query,
        key_projection_weight,
        value_projection_weight,
        q_gain,
        k_gain,
        position + PREFIX_TOKENS,
    )
    local_slot = suffix_page_map - device * pages_here
    placing = (local_slot[:, None] == jnp.arange(pages_here, dtype=jnp.int32)[None, :]).astype(
        jnp.bfloat16
    )
    both_pages = jnp.concatenate(
        [
            fresh_key_rows.reshape(pages_here, PAGE_TOKENS * HEAD_SIZE),
            fresh_value_rows.reshape(pages_here, PAGE_TOKENS * HEAD_SIZE),
        ],
        axis=1,
    )
    placed = jnp.dot(placing.T, both_pages, preferred_element_type=jnp.float32).astype(jnp.bfloat16)
    suffix_key_cache = placed[:, : PAGE_TOKENS * HEAD_SIZE].reshape(tok_count, HEAD_SIZE)
    suffix_value_cache = placed[:, PAGE_TOKENS * HEAD_SIZE :].reshape(tok_count, HEAD_SIZE)

    reach = (MAXP + pages_here - 2) // pages_here
    fresh_both = jnp.concatenate([fresh_key_rows, fresh_value_rows], axis=1)
    window = fresh_both
    covered = 1
    while covered < reach + 1:
        step = min(covered, reach + 1 - covered)
        moved = passed_along(window[: step * tok_count], "page", covered)
        window = jnp.concatenate([window, moved], axis=0)
        covered += step
    window_requests = []
    window_positions = []
    for shift_step in range(reach + 1):
        far_requests, far_position, _ = token_places(
            first_index - shift_step * tok_count, tok_count, page_lengths, request_group
        )
        window_requests.append(far_requests)
        window_positions.append(far_position)
    key_requests = jnp.concatenate(window_requests, axis=0)
    key_positions = jnp.concatenate(window_positions, axis=0)
    suffix_keys = window[:, :HEAD_SIZE]
    suffix_values = window[:, HEAD_SIZE:]

    heads = queries.shape[1]
    page_queries = queries.reshape(pages_here, PAGE_TOKENS, heads, HEAD_SIZE)
    page_requests = requests.reshape(pages_here, PAGE_TOKENS)
    page_positions = position.reshape(pages_here, PAGE_TOKENS)
    page_groups = groups.reshape(pages_here, PAGE_TOKENS)[:, 0]
    chosen = jnp.take(
        prefix_slot_map.reshape(PREFIX_COUNT, PREFIX_PAGES), page_groups, axis=0
    )
    slot_pages = every_slot.reshape(-1, PAGE_TOKENS, 2 * HEAD_SIZE)
    heads_rows = PAGE_TOKENS * heads
    kv_index = lax.axis_index("kv")
    model_width = tokens.shape[1]
    half_width = model_width // lax.axis_size("kv")

    def columns(source):
        return lax.dynamic_slice_in_dim(source, kv_index * half_width, half_width, source.ndim - 1)

    low_rank = jnp.dot(normed, laurel_left, preferred_element_type=jnp.float32).astype(jnp.bfloat16)
    laurel_full = jnp.dot(low_rank, laurel_right, preferred_element_type=jnp.float32)
    laurel = columns(normed).astype(jnp.float32) + columns(laurel_full) * rms_scale(
        laurel_full
    ) * columns(laurel_gain)
    resident = columns(tokens).astype(jnp.float32) + laurel
    head_queries = jnp.swapaxes(page_queries, 1, 2).reshape(pages_here, heads_rows, HEAD_SIZE)
    row_requests = jnp.tile(page_requests, (1, heads))[..., None]
    row_positions = jnp.tile(page_positions, (1, heads))[..., None]
    (
        resident,
        suffix_key_cache,
        suffix_value_cache,
        head_queries,
        row_requests,
        row_positions,
        suffix_keys,
        suffix_values,
    ) = lax.optimization_barrier(
        (
            resident,
            suffix_key_cache,
            suffix_value_cache,
            head_queries,
            row_requests,
            row_positions,
            suffix_keys,
            suffix_values,
        )
    )
    out_pages = []
    for p in range(pages_here):
        attn_part, attn_low = page_attention(
            chosen[p : p + 1],
            head_queries[p : p + 1],
            row_requests[p : p + 1],
            row_positions[p : p + 1],
            key_requests[None, :],
            key_positions[None, :],
            suffix_keys,
            suffix_values,
            w_out,
            slot_pages,
        )
        attn_part = attn_part.reshape(PAGE_TOKENS, model_width)
        partner_part = lax.ppermute(
            attn_low.reshape(PAGE_TOKENS, model_width), "kv", [(0, 1), (1, 0)]
        )
        summed_out = attn_part + partner_part.astype(jnp.float32)
        attn_branch = columns(summed_out) * rms_scale(summed_out) * columns(post_gain)
        rows_here = resident[p * PAGE_TOKENS : (p + 1) * PAGE_TOKENS]
        out_pages.append(((rows_here + attn_branch) * 2.0 ** (-0.5)).astype(jnp.bfloat16))
    layer_out = jnp.concatenate(out_pages, axis=0)
    return (layer_out, suffix_key_cache, suffix_value_cache)


def solution(mesh):
    placed = (
        P("page", None),
        P(),
        P(None, "kv"),
        P(None, "kv"),
        P(None, "kv"),
        P(),
        P(),
        P("kv", None),
        P(),
        P(),
        P(),
        P(),
        P("page", "kv"),
        P("page", "kv"),
        P(),
        P(),
        P(),
        P("page"),
    )
    return jax.shard_map(
        local,
        mesh=mesh,
        in_specs=placed,
        out_specs=(P("page", "kv"), P("page", "kv"), P("page", "kv")),
        check_vma=False,
    )
```

```python
import jax
import jax.numpy as jnp
from jax import lax
from jax.sharding import PartitionSpec as P
from jax.experimental import pallas as pl
from jax.experimental.pallas import tpu as pltpu

HEAD_SIZE = 256
PAGE_TOKENS = 128
PREFIX_TOKENS = 4096
PREFIX_COUNT = 4
MAXP = 8
PREFIX_PAGES = 32


epsilon = 1e-06
rope_base = 1000000.0
masked_low = -1e30


def passed_along(block, axis, distance):
    devices = range(lax.axis_size(axis))
    route = [(i - distance, i) for i in devices if i - distance in devices]
    return lax.ppermute(block, axis, route)


def rms_scale(values):
    return lax.rsqrt(jnp.mean(values * values, axis=-1, keepdims=True) + epsilon)


def rotate(values, positions):
    half_dim = values.shape[-1] // 2
    inv_freq = rope_base ** (-(jnp.arange(half_dim).astype(jnp.float32) * 2.0 / values.shape[-1]))
    angles = positions.astype(jnp.float32)[:, None] * inv_freq[None, :]
    cosine = jnp.cos(angles)[:, None, :]
    sines = jnp.sin(angles)[:, None, :]
    first_half = values[..., :half_dim]
    second_half = values[..., half_dim:]
    return jnp.concatenate(
        [first_half * cosine - second_half * sines, second_half * cosine + first_half * sines],
        axis=-1,
    )


def project(
    tokens,
    in_gain,
    w_query,
    key_projection_weight,
    value_projection_weight,
    q_gain,
    k_gain,
    positions,
):
    tok_count = tokens.shape[0]
    tokens_wide = tokens.astype(jnp.float32)
    normed = (tokens_wide * rms_scale(tokens_wide) * in_gain).astype(jnp.bfloat16)
    queries = jnp.dot(normed, w_query, preferred_element_type=jnp.float32).reshape(
        tok_count, -1, HEAD_SIZE
    )
    queries = rotate(queries * rms_scale(queries) * q_gain, positions).astype(jnp.bfloat16)
    fresh_key_rows = jnp.dot(
        normed, key_projection_weight, preferred_element_type=jnp.float32
    ).reshape(tok_count, -1, HEAD_SIZE)
    fresh_key_rows = rotate(fresh_key_rows * rms_scale(fresh_key_rows) * k_gain, positions).astype(
        jnp.bfloat16
    )
    fresh_value_rows = jnp.dot(
        normed, value_projection_weight, preferred_element_type=jnp.float32
    ).reshape(tok_count, -1, HEAD_SIZE)
    fresh_value_rows = (fresh_value_rows * rms_scale(fresh_value_rows)).astype(jnp.bfloat16)
    return (
        normed,
        queries,
        fresh_key_rows.reshape(tok_count, HEAD_SIZE),
        fresh_value_rows.reshape(tok_count, HEAD_SIZE),
    )


def token_places(first_index, tok_count, page_lengths, request_group):
    tok_ids = first_index + jnp.arange(tok_count, dtype=jnp.int32)
    page_of = tok_ids // PAGE_TOKENS
    page_starts = jnp.cumsum(page_lengths) - page_lengths
    belongs = (page_of[:, None] >= page_starts[None, :]) & (
        page_of[:, None] < (page_starts + page_lengths)[None, :]
    )
    belongs = (belongs & (tok_ids[:, None] >= 0)).astype(jnp.int32)
    request_ids = jnp.arange(page_starts.shape[0], dtype=jnp.int32)
    requests = jnp.sum(belongs * request_ids[None, :], axis=1) - (1 - jnp.sum(belongs, axis=1))
    position = tok_ids - jnp.sum(belongs * page_starts[None, :], axis=1) * PAGE_TOKENS
    groups = jnp.sum(belongs * request_group[None, :], axis=1)
    return (requests, position, groups)


def attend(queries, keys_block, values_block, key_mask):
    scores = jnp.einsum("qhd,kd->qhk", queries, keys_block, preferred_element_type=jnp.float32)
    wide_mask = key_mask[:, None, :]
    scores = jnp.where(wide_mask, scores, masked_low)
    row_top = jnp.max(scores, axis=-1)
    weights = jnp.where(wide_mask, jnp.exp(scores - row_top[..., None]), 0.0)
    row_total = jnp.sum(weights, axis=-1)
    mixture = jnp.einsum(
        "qhk,kd->qhd",
        weights.astype(jnp.bfloat16),
        values_block,
        preferred_element_type=jnp.float32,
    )
    return (row_top, row_total, mixture)


def combine(carried, incoming):
    row_top = jnp.maximum(carried[0], incoming[0])
    old_factor = jnp.exp(carried[0] - row_top)
    new_factor = jnp.exp(incoming[0] - row_top)
    row_total = carried[1] * old_factor + incoming[1] * new_factor
    mixture = carried[2] * old_factor[..., None] + incoming[2] * new_factor[..., None]
    return (row_top, row_total, mixture)


PAGES_PER_STEP = 8


def page_attention_kernel(
    table_ref, q_ref, row_req_ref, row_pos_ref, key_req_ref, key_pos_ref,
    suffix_keys_ref, suffix_values_ref, *rest,
):
    slot_refs = rest[:PAGES_PER_STEP]
    out_ref = rest[PAGES_PER_STEP]
    scores_buf, values_buf = rest[PAGES_PER_STEP + 1 :]
    step = pl.program_id(1)
    last = pl.num_programs(1) - 1
    contract_last = (((1,), (1,)), ((), ()))

    @pl.when(step < last)
    def _():
        q = q_ref[0]
        for i in range(PAGES_PER_STEP):
            page = slot_refs[i][0]
            at = pl.multiple_of((step * PAGES_PER_STEP + i) * PAGE_TOKENS, PAGE_TOKENS)
            scores_buf[:, pl.ds(at, PAGE_TOKENS)] = lax.dot_general(
                q, page[:, :HEAD_SIZE], contract_last, preferred_element_type=jnp.float32
            )
            values_buf[pl.ds(at, PAGE_TOKENS), :] = page[:, HEAD_SIZE:]

    @pl.when(step == last)
    def _():
        rows = q_ref.shape[1]
        chunk = 128
        for r in range(0, rows, chunk):
            q = q_ref[0, r : r + chunk, :]
            mask = (row_req_ref[0, r : r + chunk, :] == key_req_ref[...]) & (
                key_pos_ref[...] <= row_pos_ref[0, r : r + chunk, :]
            )
            suffix_scores = lax.dot_general(
                q, suffix_keys_ref[...], contract_last, preferred_element_type=jnp.float32
            )
            suffix_scores = jnp.where(mask, suffix_scores, masked_low)
            prefix_scores = scores_buf[r : r + chunk, :]
            row_top = jnp.maximum(
                jnp.max(prefix_scores, axis=1, keepdims=True),
                jnp.max(suffix_scores, axis=1, keepdims=True),
            )
            prefix_weights = jnp.exp(prefix_scores - row_top)
            suffix_weights = jnp.where(mask, jnp.exp(suffix_scores - row_top), 0.0)
            row_total = jnp.sum(prefix_weights, axis=1, keepdims=True) + jnp.sum(
                suffix_weights, axis=1, keepdims=True
            )
            mixture = jnp.dot(
                prefix_weights.astype(jnp.bfloat16), values_buf[...],
                preferred_element_type=jnp.float32,
            ) + jnp.dot(
                suffix_weights.astype(jnp.bfloat16), suffix_values_ref[...],
                preferred_element_type=jnp.float32,
            )
            out_ref[0, r : r + chunk, :] = (mixture / row_total).astype(out_ref.dtype)


def page_attention(table, q, row_req, row_pos, key_req, key_pos, suffix_keys, suffix_values, slot_pages):
    pages, rows, _ = q.shape
    steps = PREFIX_PAGES // PAGES_PER_STEP
    suffix_rows = suffix_keys.shape[0]

    def slot_spec(i):
        return pl.BlockSpec(
            (1, PAGE_TOKENS, 2 * HEAD_SIZE),
            lambda p, j, t, i=i: (t[p, jnp.minimum(j * PAGES_PER_STEP + i, PREFIX_PAGES - 1)], 0, 0),
        )

    grid_spec = pltpu.PrefetchScalarGridSpec(
        num_scalar_prefetch=1,
        grid=(pages, steps + 1),
        in_specs=[
            pl.BlockSpec((1, rows, HEAD_SIZE), lambda p, j, t: (p, 0, 0)),
            pl.BlockSpec((1, rows, 1), lambda p, j, t: (p, 0, 0)),
            pl.BlockSpec((1, rows, 1), lambda p, j, t: (p, 0, 0)),
            pl.BlockSpec((1, suffix_rows), lambda p, j, t: (0, 0)),
            pl.BlockSpec((1, suffix_rows), lambda p, j, t: (0, 0)),
            pl.BlockSpec((suffix_rows, HEAD_SIZE), lambda p, j, t: (0, 0)),
            pl.BlockSpec((suffix_rows, HEAD_SIZE), lambda p, j, t: (0, 0)),
        ]
        + [slot_spec(i) for i in range(PAGES_PER_STEP)],
        out_specs=pl.BlockSpec((1, rows, HEAD_SIZE), lambda p, j, t: (p, 0, 0)),
        scratch_shapes=[
            pltpu.VMEM((rows, PREFIX_PAGES * PAGE_TOKENS), jnp.float32),
            pltpu.VMEM((PREFIX_PAGES * PAGE_TOKENS, HEAD_SIZE), jnp.bfloat16),
        ],
    )
    keys_total = PREFIX_PAGES * PAGE_TOKENS + suffix_rows
    flops = pages * rows * keys_total * HEAD_SIZE * 4
    bytes_accessed = pages * (PREFIX_PAGES * PAGE_TOKENS * 2 * HEAD_SIZE * 2 + rows * HEAD_SIZE * 4)
    return pl.pallas_call(
        page_attention_kernel,
        grid_spec=grid_spec,
        out_shape=jax.ShapeDtypeStruct((pages, rows, HEAD_SIZE), jnp.bfloat16),
        compiler_params=pltpu.CompilerParams(
            dimension_semantics=("arbitrary", "arbitrary"), vmem_limit_bytes=48 * 1024 * 1024
        ),
        cost_estimate=pl.CostEstimate(
            flops=flops, transcendentals=pages * rows * keys_total, bytes_accessed=bytes_accessed
        ),
    )(table, q, row_req, row_pos, key_req, key_pos, suffix_keys, suffix_values, *([slot_pages] * PAGES_PER_STEP))


def local(
    tokens,
    in_gain,
    w_query,
    key_projection_weight,
    value_projection_weight,
    q_gain,
    k_gain,
    w_out,
    post_gain,
    laurel_left,
    laurel_right,
    laurel_gain,
    prefix_key_slots,
    prefix_value_slots,
    prefix_slot_map,
    page_lengths,
    request_group,
    suffix_page_map,
):
    tok_count = tokens.shape[0]
    pages_here = tok_count // PAGE_TOKENS
    device = lax.axis_index("page")
    first_index = device * tok_count
    prefix_both = jnp.concatenate([prefix_key_slots, prefix_value_slots], axis=1)
    every_slot = lax.all_gather(prefix_both, "page", axis=0, tiled=True)
    requests, position, groups = token_places(first_index, tok_count, page_lengths, request_group)
    normed, queries, fresh_key_rows, fresh_value_rows = project(
        tokens,
        in_gain,
        w_query,
        key_projection_weight,
        value_projection_weight,
        q_gain,
        k_gain,
        position + PREFIX_TOKENS,
    )
    local_slot = suffix_page_map - device * pages_here
    placing = (local_slot[:, None] == jnp.arange(pages_here, dtype=jnp.int32)[None, :]).astype(
        jnp.bfloat16
    )
    both_pages = jnp.concatenate(
        [
            fresh_key_rows.reshape(pages_here, PAGE_TOKENS * HEAD_SIZE),
            fresh_value_rows.reshape(pages_here, PAGE_TOKENS * HEAD_SIZE),
        ],
        axis=1,
    )
    placed = jnp.dot(placing.T, both_pages, preferred_element_type=jnp.float32).astype(jnp.bfloat16)
    suffix_key_cache = placed[:, : PAGE_TOKENS * HEAD_SIZE].reshape(tok_count, HEAD_SIZE)
    suffix_value_cache = placed[:, PAGE_TOKENS * HEAD_SIZE :].reshape(tok_count, HEAD_SIZE)

    reach = (MAXP + pages_here - 2) // pages_here
    fresh_both = jnp.concatenate([fresh_key_rows, fresh_value_rows], axis=1)
    window = fresh_both
    covered = 1
    while covered < reach + 1:
        step = min(covered, reach + 1 - covered)
        moved = passed_along(window[: step * tok_count], "page", covered)
        window = jnp.concatenate([window, moved], axis=0)
        covered += step
    window_requests = []
    window_positions = []
    for shift_step in range(reach + 1):
        far_requests, far_position, _ = token_places(
            first_index - shift_step * tok_count, tok_count, page_lengths, request_group
        )
        window_requests.append(far_requests)
        window_positions.append(far_position)
    key_requests = jnp.concatenate(window_requests, axis=0)
    key_positions = jnp.concatenate(window_positions, axis=0)
    suffix_keys = window[:, :HEAD_SIZE]
    suffix_values = window[:, HEAD_SIZE:]

    heads = queries.shape[1]
    page_queries = queries.reshape(pages_here, PAGE_TOKENS, heads, HEAD_SIZE)
    page_requests = requests.reshape(pages_here, PAGE_TOKENS)
    page_positions = position.reshape(pages_here, PAGE_TOKENS)
    page_groups = groups.reshape(pages_here, PAGE_TOKENS)[:, 0]
    chosen = jnp.take(
        prefix_slot_map.reshape(PREFIX_COUNT, PREFIX_PAGES), page_groups, axis=0
    )
    slot_pages = every_slot.reshape(-1, PAGE_TOKENS, 2 * HEAD_SIZE)
    heads_rows = PAGE_TOKENS * heads
    kv_index = lax.axis_index("kv")
    model_width = tokens.shape[1]
    half_width = model_width // lax.axis_size("kv")

    def columns(source):
        return lax.dynamic_slice_in_dim(source, kv_index * half_width, half_width, source.ndim - 1)

    low_rank = jnp.dot(normed, laurel_left, preferred_element_type=jnp.float32).astype(jnp.bfloat16)
    laurel_full = jnp.dot(low_rank, laurel_right, preferred_element_type=jnp.float32)
    laurel = columns(normed).astype(jnp.float32) + columns(laurel_full) * rms_scale(
        laurel_full
    ) * columns(laurel_gain)
    resident = columns(tokens).astype(jnp.float32) + laurel
    flat_queries = page_queries.reshape(pages_here, heads_rows, HEAD_SIZE)
    resident, suffix_key_cache, suffix_value_cache, flat_queries = lax.optimization_barrier(
        (resident, suffix_key_cache, suffix_value_cache, flat_queries)
    )
    attended = page_attention(
        chosen,
        flat_queries,
        jnp.repeat(page_requests, heads, axis=1)[..., None],
        jnp.repeat(page_positions, heads, axis=1)[..., None],
        key_requests[None, :],
        key_positions[None, :],
        suffix_keys,
        suffix_values,
        slot_pages,
    ).reshape(tok_count, -1)
    attn_part = jnp.dot(attended, w_out, preferred_element_type=jnp.float32)
    partner_part = lax.ppermute(attn_part.astype(jnp.bfloat16), "kv", [(0, 1), (1, 0)])
    summed_out = attn_part + partner_part.astype(jnp.float32)
    attn_branch = columns(summed_out) * rms_scale(summed_out) * columns(post_gain)
    layer_out = ((resident + attn_branch) * 2.0 ** (-0.5)).astype(jnp.bfloat16)
    return (layer_out, suffix_key_cache, suffix_value_cache)


def solution(mesh):
    placed = (
        P("page", None),
        P(),
        P(None, "kv"),
        P(None, "kv"),
        P(None, "kv"),
        P(),
        P(),
        P("kv", None),
        P(),
        P(),
        P(),
        P(),
        P("page", "kv"),
        P("page", "kv"),
        P(),
        P(),
        P(),
        P("page"),
    )
    return jax.shard_map(
        local,
        mesh=mesh,
        in_specs=placed,
        out_specs=(P("page", "kv"), P("page", "kv"), P("page", "kv")),
        check_vma=False,
    )
```

```python
import jax
import jax.numpy as jnp
from jax import lax
from jax.sharding import PartitionSpec as P
from jax.experimental import pallas as pl
from jax.experimental.pallas import tpu as pltpu

HEAD_SIZE = 256
PAGE_TOKENS = 128
PREFIX_TOKENS = 4096
PREFIX_COUNT = 4
MAXP = 8
PREFIX_PAGES = 32


epsilon = 1e-06
rope_base = 1000000.0
masked_low = -1e30


def passed_along(block, axis, distance):
    devices = range(lax.axis_size(axis))
    route = [(i - distance, i) for i in devices if i - distance in devices]
    return lax.ppermute(block, axis, route)


def rms_scale(values):
    return lax.rsqrt(jnp.mean(values * values, axis=-1, keepdims=True) + epsilon)


def rotate(values, positions):
    half_dim = values.shape[-1] // 2
    inv_freq = rope_base ** (-(jnp.arange(half_dim).astype(jnp.float32) * 2.0 / values.shape[-1]))
    angles = positions.astype(jnp.float32)[:, None] * inv_freq[None, :]
    cosine = jnp.cos(angles)[:, None, :]
    sines = jnp.sin(angles)[:, None, :]
    first_half = values[..., :half_dim]
    second_half = values[..., half_dim:]
    return jnp.concatenate(
        [first_half * cosine - second_half * sines, second_half * cosine + first_half * sines],
        axis=-1,
    )


def project(
    tokens,
    in_gain,
    w_query,
    key_projection_weight,
    value_projection_weight,
    q_gain,
    k_gain,
    positions,
):
    tok_count = tokens.shape[0]
    tokens_wide = tokens.astype(jnp.float32)
    normed = (tokens_wide * rms_scale(tokens_wide) * in_gain).astype(jnp.bfloat16)
    queries = jnp.dot(normed, w_query, preferred_element_type=jnp.float32).reshape(
        tok_count, -1, HEAD_SIZE
    )
    queries = rotate(queries * rms_scale(queries) * q_gain, positions).astype(jnp.bfloat16)
    fresh_key_rows = jnp.dot(
        normed, key_projection_weight, preferred_element_type=jnp.float32
    ).reshape(tok_count, -1, HEAD_SIZE)
    fresh_key_rows = rotate(fresh_key_rows * rms_scale(fresh_key_rows) * k_gain, positions).astype(
        jnp.bfloat16
    )
    fresh_value_rows = jnp.dot(
        normed, value_projection_weight, preferred_element_type=jnp.float32
    ).reshape(tok_count, -1, HEAD_SIZE)
    fresh_value_rows = (fresh_value_rows * rms_scale(fresh_value_rows)).astype(jnp.bfloat16)
    return (
        normed,
        queries,
        fresh_key_rows.reshape(tok_count, HEAD_SIZE),
        fresh_value_rows.reshape(tok_count, HEAD_SIZE),
    )


def token_places(first_index, tok_count, page_lengths, request_group):
    tok_ids = first_index + jnp.arange(tok_count, dtype=jnp.int32)
    page_of = tok_ids // PAGE_TOKENS
    page_starts = jnp.cumsum(page_lengths) - page_lengths
    belongs = (page_of[:, None] >= page_starts[None, :]) & (
        page_of[:, None] < (page_starts + page_lengths)[None, :]
    )
    belongs = (belongs & (tok_ids[:, None] >= 0)).astype(jnp.int32)
    request_ids = jnp.arange(page_starts.shape[0], dtype=jnp.int32)
    requests = jnp.sum(belongs * request_ids[None, :], axis=1) - (1 - jnp.sum(belongs, axis=1))
    position = tok_ids - jnp.sum(belongs * page_starts[None, :], axis=1) * PAGE_TOKENS
    groups = jnp.sum(belongs * request_group[None, :], axis=1)
    return (requests, position, groups)


def attend(queries, keys_block, values_block, key_mask):
    scores = jnp.einsum("qhd,kd->qhk", queries, keys_block, preferred_element_type=jnp.float32)
    wide_mask = key_mask[:, None, :]
    scores = jnp.where(wide_mask, scores, masked_low)
    row_top = jnp.max(scores, axis=-1)
    weights = jnp.where(wide_mask, jnp.exp(scores - row_top[..., None]), 0.0)
    row_total = jnp.sum(weights, axis=-1)
    mixture = jnp.einsum(
        "qhk,kd->qhd",
        weights.astype(jnp.bfloat16),
        values_block,
        preferred_element_type=jnp.float32,
    )
    return (row_top, row_total, mixture)


def combine(carried, incoming):
    row_top = jnp.maximum(carried[0], incoming[0])
    old_factor = jnp.exp(carried[0] - row_top)
    new_factor = jnp.exp(incoming[0] - row_top)
    row_total = carried[1] * old_factor + incoming[1] * new_factor
    mixture = carried[2] * old_factor[..., None] + incoming[2] * new_factor[..., None]
    return (row_top, row_total, mixture)


PAGES_PER_STEP = 8


def page_attention_kernel(
    table_ref, q_ref, row_req_ref, row_pos_ref, key_req_ref, key_pos_ref,
    suffix_keys_ref, suffix_values_ref, *rest,
):
    slot_refs = rest[:PAGES_PER_STEP]
    out_ref = rest[PAGES_PER_STEP]
    scores_buf, values_buf = rest[PAGES_PER_STEP + 1 :]
    step = pl.program_id(1)
    last = pl.num_programs(1) - 1
    contract_last = (((1,), (1,)), ((), ()))

    @pl.when(step < last)
    def _():
        q = q_ref[0]
        for i in range(PAGES_PER_STEP):
            page = slot_refs[i][0]
            at = pl.multiple_of((step * PAGES_PER_STEP + i) * PAGE_TOKENS, PAGE_TOKENS)
            scores_buf[:, pl.ds(at, PAGE_TOKENS)] = lax.dot_general(
                q, page[:, :HEAD_SIZE], contract_last, preferred_element_type=jnp.float32
            )
            values_buf[pl.ds(at, PAGE_TOKENS), :] = page[:, HEAD_SIZE:]

    @pl.when(step == last)
    def _():
        rows = q_ref.shape[1]
        chunk = 128
        for r in range(0, rows, chunk):
            q = q_ref[0, r : r + chunk, :]
            mask = (row_req_ref[0, r : r + chunk, :] == key_req_ref[...]) & (
                key_pos_ref[...] <= row_pos_ref[0, r : r + chunk, :]
            )
            suffix_scores = lax.dot_general(
                q, suffix_keys_ref[...], contract_last, preferred_element_type=jnp.float32
            )
            suffix_scores = jnp.where(mask, suffix_scores, masked_low)
            prefix_scores = scores_buf[r : r + chunk, :]
            row_top = jnp.maximum(
                jnp.max(prefix_scores, axis=1, keepdims=True),
                jnp.max(suffix_scores, axis=1, keepdims=True),
            )
            prefix_weights = jnp.exp(prefix_scores - row_top)
            suffix_weights = jnp.where(mask, jnp.exp(suffix_scores - row_top), 0.0)
            row_total = jnp.sum(prefix_weights, axis=1, keepdims=True) + jnp.sum(
                suffix_weights, axis=1, keepdims=True
            )
            mixture = jnp.dot(
                prefix_weights.astype(jnp.bfloat16), values_buf[...],
                preferred_element_type=jnp.float32,
            ) + jnp.dot(
                suffix_weights.astype(jnp.bfloat16), suffix_values_ref[...],
                preferred_element_type=jnp.float32,
            )
            out_ref[0, :, r * 2 : r * 2 + HEAD_SIZE] = (mixture / row_total).astype(out_ref.dtype)


def page_attention(table, q, row_req, row_pos, key_req, key_pos, suffix_keys, suffix_values, slot_pages):
    pages, rows, _ = q.shape
    steps = PREFIX_PAGES // PAGES_PER_STEP
    suffix_rows = suffix_keys.shape[0]

    def slot_spec(i):
        return pl.BlockSpec(
            (1, PAGE_TOKENS, 2 * HEAD_SIZE),
            lambda p, j, t, i=i: (t[p, jnp.minimum(j * PAGES_PER_STEP + i, PREFIX_PAGES - 1)], 0, 0),
        )

    grid_spec = pltpu.PrefetchScalarGridSpec(
        num_scalar_prefetch=1,
        grid=(pages, steps + 1),
        in_specs=[
            pl.BlockSpec((1, rows, HEAD_SIZE), lambda p, j, t: (p, 0, 0)),
            pl.BlockSpec((1, rows, 1), lambda p, j, t: (p, 0, 0)),
            pl.BlockSpec((1, rows, 1), lambda p, j, t: (p, 0, 0)),
            pl.BlockSpec((1, suffix_rows), lambda p, j, t: (0, 0)),
            pl.BlockSpec((1, suffix_rows), lambda p, j, t: (0, 0)),
            pl.BlockSpec((suffix_rows, HEAD_SIZE), lambda p, j, t: (0, 0)),
            pl.BlockSpec((suffix_rows, HEAD_SIZE), lambda p, j, t: (0, 0)),
        ]
        + [slot_spec(i) for i in range(PAGES_PER_STEP)],
        out_specs=pl.BlockSpec((1, PAGE_TOKENS, rows // PAGE_TOKENS * HEAD_SIZE), lambda p, j, t: (p, 0, 0)),
        scratch_shapes=[
            pltpu.VMEM((rows, PREFIX_PAGES * PAGE_TOKENS), jnp.float32),
            pltpu.VMEM((PREFIX_PAGES * PAGE_TOKENS, HEAD_SIZE), jnp.bfloat16),
        ],
    )
    keys_total = PREFIX_PAGES * PAGE_TOKENS + suffix_rows
    flops = pages * rows * keys_total * HEAD_SIZE * 4
    bytes_accessed = pages * (PREFIX_PAGES * PAGE_TOKENS * 2 * HEAD_SIZE * 2 + rows * HEAD_SIZE * 4)
    return pl.pallas_call(
        page_attention_kernel,
        grid_spec=grid_spec,
        out_shape=jax.ShapeDtypeStruct((pages, PAGE_TOKENS, rows // PAGE_TOKENS * HEAD_SIZE), jnp.bfloat16),
        compiler_params=pltpu.CompilerParams(
            dimension_semantics=("arbitrary", "arbitrary"), vmem_limit_bytes=48 * 1024 * 1024
        ),
        cost_estimate=pl.CostEstimate(
            flops=flops, transcendentals=pages * rows * keys_total, bytes_accessed=bytes_accessed
        ),
    )(table, q, row_req, row_pos, key_req, key_pos, suffix_keys, suffix_values, *([slot_pages] * PAGES_PER_STEP))


def local(
    tokens,
    in_gain,
    w_query,
    key_projection_weight,
    value_projection_weight,
    q_gain,
    k_gain,
    w_out,
    post_gain,
    laurel_left,
    laurel_right,
    laurel_gain,
    prefix_key_slots,
    prefix_value_slots,
    prefix_slot_map,
    page_lengths,
    request_group,
    suffix_page_map,
):
    tok_count = tokens.shape[0]
    pages_here = tok_count // PAGE_TOKENS
    device = lax.axis_index("page")
    first_index = device * tok_count
    prefix_both = jnp.concatenate([prefix_key_slots, prefix_value_slots], axis=1)
    every_slot = lax.all_gather(prefix_both, "page", axis=0, tiled=True)
    requests, position, groups = token_places(first_index, tok_count, page_lengths, request_group)
    normed, queries, fresh_key_rows, fresh_value_rows = project(
        tokens,
        in_gain,
        w_query,
        key_projection_weight,
        value_projection_weight,
        q_gain,
        k_gain,
        position + PREFIX_TOKENS,
    )
    local_slot = suffix_page_map - device * pages_here
    placing = (local_slot[:, None] == jnp.arange(pages_here, dtype=jnp.int32)[None, :]).astype(
        jnp.bfloat16
    )
    both_pages = jnp.concatenate(
        [
            fresh_key_rows.reshape(pages_here, PAGE_TOKENS * HEAD_SIZE),
            fresh_value_rows.reshape(pages_here, PAGE_TOKENS * HEAD_SIZE),
        ],
        axis=1,
    )
    placed = jnp.dot(placing.T, both_pages, preferred_element_type=jnp.float32).astype(jnp.bfloat16)
    suffix_key_cache = placed[:, : PAGE_TOKENS * HEAD_SIZE].reshape(tok_count, HEAD_SIZE)
    suffix_value_cache = placed[:, PAGE_TOKENS * HEAD_SIZE :].reshape(tok_count, HEAD_SIZE)

    reach = (MAXP + pages_here - 2) // pages_here
    fresh_both = jnp.concatenate([fresh_key_rows, fresh_value_rows], axis=1)
    window = fresh_both
    covered = 1
    while covered < reach + 1:
        step = min(covered, reach + 1 - covered)
        moved = passed_along(window[: step * tok_count], "page", covered)
        window = jnp.concatenate([window, moved], axis=0)
        covered += step
    window_requests = []
    window_positions = []
    for shift_step in range(reach + 1):
        far_requests, far_position, _ = token_places(
            first_index - shift_step * tok_count, tok_count, page_lengths, request_group
        )
        window_requests.append(far_requests)
        window_positions.append(far_position)
    key_requests = jnp.concatenate(window_requests, axis=0)
    key_positions = jnp.concatenate(window_positions, axis=0)
    suffix_keys = window[:, :HEAD_SIZE]
    suffix_values = window[:, HEAD_SIZE:]

    heads = queries.shape[1]
    page_queries = queries.reshape(pages_here, PAGE_TOKENS, heads, HEAD_SIZE)
    page_requests = requests.reshape(pages_here, PAGE_TOKENS)
    page_positions = position.reshape(pages_here, PAGE_TOKENS)
    page_groups = groups.reshape(pages_here, PAGE_TOKENS)[:, 0]
    chosen = jnp.take(
        prefix_slot_map.reshape(PREFIX_COUNT, PREFIX_PAGES), page_groups, axis=0
    )
    slot_pages = every_slot.reshape(-1, PAGE_TOKENS, 2 * HEAD_SIZE)
    heads_rows = PAGE_TOKENS * heads
    kv_index = lax.axis_index("kv")
    model_width = tokens.shape[1]
    half_width = model_width // lax.axis_size("kv")

    def columns(source):
        return lax.dynamic_slice_in_dim(source, kv_index * half_width, half_width, source.ndim - 1)

    low_rank = jnp.dot(normed, laurel_left, preferred_element_type=jnp.float32).astype(jnp.bfloat16)
    laurel_full = jnp.dot(low_rank, laurel_right, preferred_element_type=jnp.float32)
    laurel = columns(normed).astype(jnp.float32) + columns(laurel_full) * rms_scale(
        laurel_full
    ) * columns(laurel_gain)
    resident = columns(tokens).astype(jnp.float32) + laurel
    flat_queries = jnp.swapaxes(page_queries, 1, 2).reshape(pages_here, heads_rows, HEAD_SIZE)
    resident, suffix_key_cache, suffix_value_cache, flat_queries = lax.optimization_barrier(
        (resident, suffix_key_cache, suffix_value_cache, flat_queries)
    )
    attended = page_attention(
        chosen,
        flat_queries,
        jnp.tile(page_requests, (1, heads))[..., None],
        jnp.tile(page_positions, (1, heads))[..., None],
        key_requests[None, :],
        key_positions[None, :],
        suffix_keys,
        suffix_values,
        slot_pages,
    ).reshape(tok_count, -1)
    attn_part = jnp.dot(attended, w_out, preferred_element_type=jnp.float32)
    partner_part = lax.ppermute(attn_part.astype(jnp.bfloat16), "kv", [(0, 1), (1, 0)])
    summed_out = attn_part + partner_part.astype(jnp.float32)
    attn_branch = columns(summed_out) * rms_scale(summed_out) * columns(post_gain)
    layer_out = ((resident + attn_branch) * 2.0 ** (-0.5)).astype(jnp.bfloat16)
    return (layer_out, suffix_key_cache, suffix_value_cache)


def solution(mesh):
    placed = (
        P("page", None),
        P(),
        P(None, "kv"),
        P(None, "kv"),
        P(None, "kv"),
        P(),
        P(),
        P("kv", None),
        P(),
        P(),
        P(),
        P(),
        P("page", "kv"),
        P("page", "kv"),
        P(),
        P(),
        P(),
        P("page"),
    )
    return jax.shard_map(
        local,
        mesh=mesh,
        in_specs=placed,
        out_specs=(P("page", "kv"), P("page", "kv"), P("page", "kv")),
        check_vma=False,
    )
```

```python
import jax
import jax.numpy as jnp
from jax import lax
from jax.sharding import PartitionSpec as P
from jax.experimental import pallas as pl
from jax.experimental.pallas import tpu as pltpu

HEAD_SIZE = 256
PAGE_TOKENS = 128
PREFIX_TOKENS = 4096
PREFIX_COUNT = 4
MAXP = 8
PREFIX_PAGES = 32


epsilon = 1e-06
rope_base = 1000000.0
masked_low = -1e30


def passed_along(block, axis, distance):
    devices = range(lax.axis_size(axis))
    route = [(i - distance, i) for i in devices if i - distance in devices]
    return lax.ppermute(block, axis, route)


def rms_scale(values):
    return lax.rsqrt(jnp.mean(values * values, axis=-1, keepdims=True) + epsilon)


def rotate(values, positions):
    half_dim = values.shape[-1] // 2
    inv_freq = rope_base ** (-(jnp.arange(half_dim).astype(jnp.float32) * 2.0 / values.shape[-1]))
    angles = positions.astype(jnp.float32)[:, None] * inv_freq[None, :]
    cosine = jnp.cos(angles)[:, None, :]
    sines = jnp.sin(angles)[:, None, :]
    first_half = values[..., :half_dim]
    second_half = values[..., half_dim:]
    return jnp.concatenate(
        [first_half * cosine - second_half * sines, second_half * cosine + first_half * sines],
        axis=-1,
    )


def project(
    tokens,
    in_gain,
    w_query,
    key_projection_weight,
    value_projection_weight,
    q_gain,
    k_gain,
    positions,
):
    tok_count = tokens.shape[0]
    tokens_wide = tokens.astype(jnp.float32)
    normed = (tokens_wide * rms_scale(tokens_wide) * in_gain).astype(jnp.bfloat16)
    queries = jnp.dot(normed, w_query, preferred_element_type=jnp.float32).reshape(
        tok_count, -1, HEAD_SIZE
    )
    queries = rotate(queries * rms_scale(queries) * q_gain, positions).astype(jnp.bfloat16)
    fresh_key_rows = jnp.dot(
        normed, key_projection_weight, preferred_element_type=jnp.float32
    ).reshape(tok_count, -1, HEAD_SIZE)
    fresh_key_rows = rotate(fresh_key_rows * rms_scale(fresh_key_rows) * k_gain, positions).astype(
        jnp.bfloat16
    )
    fresh_value_rows = jnp.dot(
        normed, value_projection_weight, preferred_element_type=jnp.float32
    ).reshape(tok_count, -1, HEAD_SIZE)
    fresh_value_rows = (fresh_value_rows * rms_scale(fresh_value_rows)).astype(jnp.bfloat16)
    return (
        normed,
        queries,
        fresh_key_rows.reshape(tok_count, HEAD_SIZE),
        fresh_value_rows.reshape(tok_count, HEAD_SIZE),
    )


def token_places(first_index, tok_count, page_lengths, request_group):
    tok_ids = first_index + jnp.arange(tok_count, dtype=jnp.int32)
    page_of = tok_ids // PAGE_TOKENS
    page_starts = jnp.cumsum(page_lengths) - page_lengths
    belongs = (page_of[:, None] >= page_starts[None, :]) & (
        page_of[:, None] < (page_starts + page_lengths)[None, :]
    )
    belongs = (belongs & (tok_ids[:, None] >= 0)).astype(jnp.int32)
    request_ids = jnp.arange(page_starts.shape[0], dtype=jnp.int32)
    requests = jnp.sum(belongs * request_ids[None, :], axis=1) - (1 - jnp.sum(belongs, axis=1))
    position = tok_ids - jnp.sum(belongs * page_starts[None, :], axis=1) * PAGE_TOKENS
    groups = jnp.sum(belongs * request_group[None, :], axis=1)
    return (requests, position, groups)


def attend(queries, keys_block, values_block, key_mask):
    scores = jnp.einsum("qhd,kd->qhk", queries, keys_block, preferred_element_type=jnp.float32)
    wide_mask = key_mask[:, None, :]
    scores = jnp.where(wide_mask, scores, masked_low)
    row_top = jnp.max(scores, axis=-1)
    weights = jnp.where(wide_mask, jnp.exp(scores - row_top[..., None]), 0.0)
    row_total = jnp.sum(weights, axis=-1)
    mixture = jnp.einsum(
        "qhk,kd->qhd",
        weights.astype(jnp.bfloat16),
        values_block,
        preferred_element_type=jnp.float32,
    )
    return (row_top, row_total, mixture)


def combine(carried, incoming):
    row_top = jnp.maximum(carried[0], incoming[0])
    old_factor = jnp.exp(carried[0] - row_top)
    new_factor = jnp.exp(incoming[0] - row_top)
    row_total = carried[1] * old_factor + incoming[1] * new_factor
    mixture = carried[2] * old_factor[..., None] + incoming[2] * new_factor[..., None]
    return (row_top, row_total, mixture)


PAGES_PER_STEP = 8


def page_attention_kernel(
    table_ref, q_ref, row_req_ref, row_pos_ref, key_req_ref, key_pos_ref,
    suffix_keys_ref, suffix_values_ref, *rest,
):
    slot_refs = rest[:PAGES_PER_STEP]
    out_ref = rest[PAGES_PER_STEP]
    scores_buf, values_buf, stage_buf = rest[PAGES_PER_STEP + 1 :]
    step = pl.program_id(1)
    last = pl.num_programs(1) - 1
    contract_last = (((1,), (1,)), ((), ()))

    @pl.when(step < last)
    def _():
        q = q_ref[0]
        for i in range(PAGES_PER_STEP):
            page = slot_refs[i][0]
            at = pl.multiple_of((step * PAGES_PER_STEP + i) * PAGE_TOKENS, PAGE_TOKENS)
            scores_buf[:, pl.ds(at, PAGE_TOKENS)] = lax.dot_general(
                q, page[:, :HEAD_SIZE], contract_last, preferred_element_type=jnp.float32
            )
            values_buf[pl.ds(at, PAGE_TOKENS), :] = page[:, HEAD_SIZE:]

    @pl.when(step == last)
    def _():
        rows = q_ref.shape[1]
        chunk = 128
        for r in range(0, rows, chunk):
            q = q_ref[0, r : r + chunk, :]
            mask = (row_req_ref[0, r : r + chunk, :] == key_req_ref[...]) & (
                key_pos_ref[...] <= row_pos_ref[0, r : r + chunk, :]
            )
            suffix_scores = lax.dot_general(
                q, suffix_keys_ref[...], contract_last, preferred_element_type=jnp.float32
            )
            suffix_scores = jnp.where(mask, suffix_scores, masked_low)
            prefix_scores = scores_buf[r : r + chunk, :]
            row_top = jnp.maximum(
                jnp.max(prefix_scores, axis=1, keepdims=True),
                jnp.max(suffix_scores, axis=1, keepdims=True),
            )
            prefix_weights = jnp.exp(prefix_scores - row_top)
            suffix_weights = jnp.where(mask, jnp.exp(suffix_scores - row_top), 0.0)
            row_total = jnp.sum(prefix_weights, axis=1, keepdims=True) + jnp.sum(
                suffix_weights, axis=1, keepdims=True
            )
            mixture = jnp.dot(
                prefix_weights.astype(jnp.bfloat16), values_buf[...],
                preferred_element_type=jnp.float32,
            ) + jnp.dot(
                suffix_weights.astype(jnp.bfloat16), suffix_values_ref[...],
                preferred_element_type=jnp.float32,
            )
            result = mixture / row_total
            lanes = 128
            halves = HEAD_SIZE // lanes
            for c in range(halves):
                stage_buf[c] = result[:, c * lanes : (c + 1) * lanes]
            heads = out_ref.shape[2] // HEAD_SIZE
            tokens_here = chunk // heads
            for h in range(heads):
                for c in range(halves):
                    out_ref[0, pl.ds(r // heads, tokens_here), pl.ds(h * HEAD_SIZE + c * lanes, lanes)] = stage_buf[
                        c, pl.ds(h, tokens_here, stride=heads), :
                    ].astype(out_ref.dtype)


def page_attention(table, q, row_req, row_pos, key_req, key_pos, suffix_keys, suffix_values, slot_pages):
    pages, rows, _ = q.shape
    steps = PREFIX_PAGES // PAGES_PER_STEP
    suffix_rows = suffix_keys.shape[0]

    def slot_spec(i):
        return pl.BlockSpec(
            (1, PAGE_TOKENS, 2 * HEAD_SIZE),
            lambda p, j, t, i=i: (t[p, jnp.minimum(j * PAGES_PER_STEP + i, PREFIX_PAGES - 1)], 0, 0),
        )

    grid_spec = pltpu.PrefetchScalarGridSpec(
        num_scalar_prefetch=1,
        grid=(pages, steps + 1),
        in_specs=[
            pl.BlockSpec((1, rows, HEAD_SIZE), lambda p, j, t: (p, 0, 0)),
            pl.BlockSpec((1, rows, 1), lambda p, j, t: (p, 0, 0)),
            pl.BlockSpec((1, rows, 1), lambda p, j, t: (p, 0, 0)),
            pl.BlockSpec((1, suffix_rows), lambda p, j, t: (0, 0)),
            pl.BlockSpec((1, suffix_rows), lambda p, j, t: (0, 0)),
            pl.BlockSpec((suffix_rows, HEAD_SIZE), lambda p, j, t: (0, 0)),
            pl.BlockSpec((suffix_rows, HEAD_SIZE), lambda p, j, t: (0, 0)),
        ]
        + [slot_spec(i) for i in range(PAGES_PER_STEP)],
        out_specs=pl.BlockSpec((1, PAGE_TOKENS, rows // PAGE_TOKENS * HEAD_SIZE), lambda p, j, t: (p, 0, 0)),
        scratch_shapes=[
            pltpu.VMEM((rows, PREFIX_PAGES * PAGE_TOKENS), jnp.float32),
            pltpu.VMEM((PREFIX_PAGES * PAGE_TOKENS, HEAD_SIZE), jnp.bfloat16),
            pltpu.VMEM((HEAD_SIZE // 128, 128, 128), jnp.float32),
        ],
    )
    keys_total = PREFIX_PAGES * PAGE_TOKENS + suffix_rows
    flops = pages * rows * keys_total * HEAD_SIZE * 4
    bytes_accessed = pages * (PREFIX_PAGES * PAGE_TOKENS * 2 * HEAD_SIZE * 2 + rows * HEAD_SIZE * 4)
    return pl.pallas_call(
        page_attention_kernel,
        grid_spec=grid_spec,
        out_shape=jax.ShapeDtypeStruct((pages, PAGE_TOKENS, rows // PAGE_TOKENS * HEAD_SIZE), jnp.bfloat16),
        compiler_params=pltpu.CompilerParams(
            dimension_semantics=("arbitrary", "arbitrary"), vmem_limit_bytes=48 * 1024 * 1024
        ),
        cost_estimate=pl.CostEstimate(
            flops=flops, transcendentals=pages * rows * keys_total, bytes_accessed=bytes_accessed
        ),
    )(table, q, row_req, row_pos, key_req, key_pos, suffix_keys, suffix_values, *([slot_pages] * PAGES_PER_STEP))


def local(
    tokens,
    in_gain,
    w_query,
    key_projection_weight,
    value_projection_weight,
    q_gain,
    k_gain,
    w_out,
    post_gain,
    laurel_left,
    laurel_right,
    laurel_gain,
    prefix_key_slots,
    prefix_value_slots,
    prefix_slot_map,
    page_lengths,
    request_group,
    suffix_page_map,
):
    tok_count = tokens.shape[0]
    pages_here = tok_count // PAGE_TOKENS
    device = lax.axis_index("page")
    first_index = device * tok_count
    prefix_both = jnp.concatenate([prefix_key_slots, prefix_value_slots], axis=1)
    every_slot = lax.all_gather(prefix_both, "page", axis=0, tiled=True)
    requests, position, groups = token_places(first_index, tok_count, page_lengths, request_group)
    normed, queries, fresh_key_rows, fresh_value_rows = project(
        tokens,
        in_gain,
        w_query,
        key_projection_weight,
        value_projection_weight,
        q_gain,
        k_gain,
        position + PREFIX_TOKENS,
    )
    local_slot = suffix_page_map - device * pages_here
    placing = (local_slot[:, None] == jnp.arange(pages_here, dtype=jnp.int32)[None, :]).astype(
        jnp.bfloat16
    )
    both_pages = jnp.concatenate(
        [
            fresh_key_rows.reshape(pages_here, PAGE_TOKENS * HEAD_SIZE),
            fresh_value_rows.reshape(pages_here, PAGE_TOKENS * HEAD_SIZE),
        ],
        axis=1,
    )
    placed = jnp.dot(placing.T, both_pages, preferred_element_type=jnp.float32).astype(jnp.bfloat16)
    suffix_key_cache = placed[:, : PAGE_TOKENS * HEAD_SIZE].reshape(tok_count, HEAD_SIZE)
    suffix_value_cache = placed[:, PAGE_TOKENS * HEAD_SIZE :].reshape(tok_count, HEAD_SIZE)

    reach = (MAXP + pages_here - 2) // pages_here
    fresh_both = jnp.concatenate([fresh_key_rows, fresh_value_rows], axis=1)
    window = fresh_both
    covered = 1
    while covered < reach + 1:
        step = min(covered, reach + 1 - covered)
        moved = passed_along(window[: step * tok_count], "page", covered)
        window = jnp.concatenate([window, moved], axis=0)
        covered += step
    window_requests = []
    window_positions = []
    for shift_step in range(reach + 1):
        far_requests, far_position, _ = token_places(
            first_index - shift_step * tok_count, tok_count, page_lengths, request_group
        )
        window_requests.append(far_requests)
        window_positions.append(far_position)
    key_requests = jnp.concatenate(window_requests, axis=0)
    key_positions = jnp.concatenate(window_positions, axis=0)
    suffix_keys = window[:, :HEAD_SIZE]
    suffix_values = window[:, HEAD_SIZE:]

    heads = queries.shape[1]
    page_queries = queries.reshape(pages_here, PAGE_TOKENS, heads, HEAD_SIZE)
    page_requests = requests.reshape(pages_here, PAGE_TOKENS)
    page_positions = position.reshape(pages_here, PAGE_TOKENS)
    page_groups = groups.reshape(pages_here, PAGE_TOKENS)[:, 0]
    chosen = jnp.take(
        prefix_slot_map.reshape(PREFIX_COUNT, PREFIX_PAGES), page_groups, axis=0
    )
    slot_pages = every_slot.reshape(-1, PAGE_TOKENS, 2 * HEAD_SIZE)
    heads_rows = PAGE_TOKENS * heads
    kv_index = lax.axis_index("kv")
    model_width = tokens.shape[1]
    half_width = model_width // lax.axis_size("kv")

    def columns(source):
        return lax.dynamic_slice_in_dim(source, kv_index * half_width, half_width, source.ndim - 1)

    low_rank = jnp.dot(normed, laurel_left, preferred_element_type=jnp.float32).astype(jnp.bfloat16)
    laurel_full = jnp.dot(low_rank, laurel_right, preferred_element_type=jnp.float32)
    laurel = columns(normed).astype(jnp.float32) + columns(laurel_full) * rms_scale(
        laurel_full
    ) * columns(laurel_gain)
    resident = columns(tokens).astype(jnp.float32) + laurel
    flat_queries = page_queries.reshape(pages_here, heads_rows, HEAD_SIZE)
    resident, suffix_key_cache, suffix_value_cache, flat_queries = lax.optimization_barrier(
        (resident, suffix_key_cache, suffix_value_cache, flat_queries)
    )
    attended = page_attention(
        chosen,
        flat_queries,
        jnp.repeat(page_requests, heads, axis=1)[..., None],
        jnp.repeat(page_positions, heads, axis=1)[..., None],
        key_requests[None, :],
        key_positions[None, :],
        suffix_keys,
        suffix_values,
        slot_pages,
    ).reshape(tok_count, -1)
    attn_part = jnp.dot(attended, w_out, preferred_element_type=jnp.float32)
    partner_part = lax.ppermute(attn_part.astype(jnp.bfloat16), "kv", [(0, 1), (1, 0)])
    summed_out = attn_part + partner_part.astype(jnp.float32)
    attn_branch = columns(summed_out) * rms_scale(summed_out) * columns(post_gain)
    layer_out = ((resident + attn_branch) * 2.0 ** (-0.5)).astype(jnp.bfloat16)
    return (layer_out, suffix_key_cache, suffix_value_cache)


def solution(mesh):
    placed = (
        P("page", None),
        P(),
        P(None, "kv"),
        P(None, "kv"),
        P(None, "kv"),
        P(),
        P(),
        P("kv", None),
        P(),
        P(),
        P(),
        P(),
        P("page", "kv"),
        P("page", "kv"),
        P(),
        P(),
        P(),
        P("page"),
    )
    return jax.shard_map(
        local,
        mesh=mesh,
        in_specs=placed,
        out_specs=(P("page", "kv"), P("page", "kv"), P("page", "kv")),
        check_vma=False,
    )
```

```python
import jax
import jax.numpy as jnp
from jax import lax
from jax.sharding import PartitionSpec as P
from jax.experimental import pallas as pl
from jax.experimental.pallas import tpu as pltpu

HEAD_SIZE = 256
PAGE_TOKENS = 128
PREFIX_TOKENS = 4096
PREFIX_COUNT = 4
MAXP = 8
PREFIX_PAGES = 32


epsilon = 1e-06
rope_base = 1000000.0
masked_low = -1e30


def passed_along(block, axis, distance):
    devices = range(lax.axis_size(axis))
    route = [(i - distance, i) for i in devices if i - distance in devices]
    return lax.ppermute(block, axis, route)


def rms_scale(values):
    return lax.rsqrt(jnp.mean(values * values, axis=-1, keepdims=True) + epsilon)


def rotate(values, positions):
    half_dim = values.shape[-1] // 2
    inv_freq = rope_base ** (-(jnp.arange(half_dim).astype(jnp.float32) * 2.0 / values.shape[-1]))
    angles = positions.astype(jnp.float32)[:, None] * inv_freq[None, :]
    cosine = jnp.cos(angles)[:, None, :]
    sines = jnp.sin(angles)[:, None, :]
    first_half = values[..., :half_dim]
    second_half = values[..., half_dim:]
    return jnp.concatenate(
        [first_half * cosine - second_half * sines, second_half * cosine + first_half * sines],
        axis=-1,
    )


def project(
    tokens,
    in_gain,
    w_query,
    key_projection_weight,
    value_projection_weight,
    q_gain,
    k_gain,
    positions,
):
    tok_count = tokens.shape[0]
    tokens_wide = tokens.astype(jnp.float32)
    normed = (tokens_wide * rms_scale(tokens_wide) * in_gain).astype(jnp.bfloat16)
    queries = jnp.dot(normed, w_query, preferred_element_type=jnp.float32).reshape(
        tok_count, -1, HEAD_SIZE
    )
    queries = rotate(queries * rms_scale(queries) * q_gain, positions).astype(jnp.bfloat16)
    fresh_key_rows = jnp.dot(
        normed, key_projection_weight, preferred_element_type=jnp.float32
    ).reshape(tok_count, -1, HEAD_SIZE)
    fresh_key_rows = rotate(fresh_key_rows * rms_scale(fresh_key_rows) * k_gain, positions).astype(
        jnp.bfloat16
    )
    fresh_value_rows = jnp.dot(
        normed, value_projection_weight, preferred_element_type=jnp.float32
    ).reshape(tok_count, -1, HEAD_SIZE)
    fresh_value_rows = (fresh_value_rows * rms_scale(fresh_value_rows)).astype(jnp.bfloat16)
    return (
        normed,
        queries,
        fresh_key_rows.reshape(tok_count, HEAD_SIZE),
        fresh_value_rows.reshape(tok_count, HEAD_SIZE),
    )


def token_places(first_index, tok_count, page_lengths, request_group):
    tok_ids = first_index + jnp.arange(tok_count, dtype=jnp.int32)
    page_of = tok_ids // PAGE_TOKENS
    page_starts = jnp.cumsum(page_lengths) - page_lengths
    belongs = (page_of[:, None] >= page_starts[None, :]) & (
        page_of[:, None] < (page_starts + page_lengths)[None, :]
    )
    belongs = (belongs & (tok_ids[:, None] >= 0)).astype(jnp.int32)
    request_ids = jnp.arange(page_starts.shape[0], dtype=jnp.int32)
    requests = jnp.sum(belongs * request_ids[None, :], axis=1) - (1 - jnp.sum(belongs, axis=1))
    position = tok_ids - jnp.sum(belongs * page_starts[None, :], axis=1) * PAGE_TOKENS
    groups = jnp.sum(belongs * request_group[None, :], axis=1)
    return (requests, position, groups)


def attend(queries, keys_block, values_block, key_mask):
    scores = jnp.einsum("qhd,kd->qhk", queries, keys_block, preferred_element_type=jnp.float32)
    wide_mask = key_mask[:, None, :]
    scores = jnp.where(wide_mask, scores, masked_low)
    row_top = jnp.max(scores, axis=-1)
    weights = jnp.where(wide_mask, jnp.exp(scores - row_top[..., None]), 0.0)
    row_total = jnp.sum(weights, axis=-1)
    mixture = jnp.einsum(
        "qhk,kd->qhd",
        weights.astype(jnp.bfloat16),
        values_block,
        preferred_element_type=jnp.float32,
    )
    return (row_top, row_total, mixture)


def combine(carried, incoming):
    row_top = jnp.maximum(carried[0], incoming[0])
    old_factor = jnp.exp(carried[0] - row_top)
    new_factor = jnp.exp(incoming[0] - row_top)
    row_total = carried[1] * old_factor + incoming[1] * new_factor
    mixture = carried[2] * old_factor[..., None] + incoming[2] * new_factor[..., None]
    return (row_top, row_total, mixture)


PAGES_PER_STEP = 8


def page_attention_kernel(
    table_ref, q_ref, row_req_ref, row_pos_ref, key_req_ref, key_pos_ref,
    suffix_keys_ref, suffix_values_ref, *rest,
):
    slot_refs = rest[:PAGES_PER_STEP]
    out_ref = rest[PAGES_PER_STEP]
    scores_buf, values_buf, stage_buf = rest[PAGES_PER_STEP + 1 :]
    step = pl.program_id(1)
    last = pl.num_programs(1) - 1
    contract_last = (((1,), (1,)), ((), ()))

    @pl.when(step < last)
    def _():
        q = q_ref[0]
        for i in range(PAGES_PER_STEP):
            page = slot_refs[i][0]
            at = pl.multiple_of((step * PAGES_PER_STEP + i) * PAGE_TOKENS, PAGE_TOKENS)
            scores_buf[:, pl.ds(at, PAGE_TOKENS)] = lax.dot_general(
                q, page[:, :HEAD_SIZE], contract_last, preferred_element_type=jnp.float32
            )
            values_buf[pl.ds(at, PAGE_TOKENS), :] = page[:, HEAD_SIZE:]

    @pl.when(step == last)
    def _():
        rows = q_ref.shape[1]
        chunk = 128
        for r in range(0, rows, chunk):
            q = q_ref[0, r : r + chunk, :]
            mask = (row_req_ref[0, r : r + chunk, :] == key_req_ref[...]) & (
                key_pos_ref[...] <= row_pos_ref[0, r : r + chunk, :]
            )
            suffix_scores = lax.dot_general(
                q, suffix_keys_ref[...], contract_last, preferred_element_type=jnp.float32
            )
            suffix_scores = jnp.where(mask, suffix_scores, masked_low)
            prefix_scores = scores_buf[r : r + chunk, :]
            row_top = jnp.maximum(
                jnp.max(prefix_scores, axis=1, keepdims=True),
                jnp.max(suffix_scores, axis=1, keepdims=True),
            )
            prefix_weights = jnp.exp(prefix_scores - row_top)
            suffix_weights = jnp.where(mask, jnp.exp(suffix_scores - row_top), 0.0)
            row_total = jnp.sum(prefix_weights, axis=1, keepdims=True) + jnp.sum(
                suffix_weights, axis=1, keepdims=True
            )
            mixture = jnp.dot(
                prefix_weights.astype(jnp.bfloat16), values_buf[...],
                preferred_element_type=jnp.float32,
            ) + jnp.dot(
                suffix_weights.astype(jnp.bfloat16), suffix_values_ref[...],
                preferred_element_type=jnp.float32,
            )
            result = mixture / row_total
            lanes = 128
            halves = HEAD_SIZE // lanes
            for c in range(halves):
                stage_buf[c] = result[:, c * lanes : (c + 1) * lanes]
            heads = out_ref.shape[2] // HEAD_SIZE
            tokens_here = chunk // heads
            for h in range(heads):
                for c in range(halves):
                    out_ref[0, pl.ds(r // heads, tokens_here), pl.ds(h * HEAD_SIZE + c * lanes, lanes)] = stage_buf[
                        c, pl.ds(h, tokens_here, stride=heads), :
                    ].astype(out_ref.dtype)


def page_attention(table, q, row_req, row_pos, key_req, key_pos, suffix_keys, suffix_values, slot_pages):
    pages, rows, _ = q.shape
    steps = PREFIX_PAGES // PAGES_PER_STEP
    suffix_rows = suffix_keys.shape[0]

    def slot_spec(i):
        return pl.BlockSpec(
            (1, PAGE_TOKENS, 2 * HEAD_SIZE),
            lambda p, j, t, i=i: (t[p, jnp.minimum(j * PAGES_PER_STEP + i, PREFIX_PAGES - 1)], 0, 0),
        )

    grid_spec = pltpu.PrefetchScalarGridSpec(
        num_scalar_prefetch=1,
        grid=(pages, steps + 1),
        in_specs=[
            pl.BlockSpec((1, rows, HEAD_SIZE), lambda p, j, t: (p, 0, 0)),
            pl.BlockSpec((1, rows, 1), lambda p, j, t: (p, 0, 0)),
            pl.BlockSpec((1, rows, 1), lambda p, j, t: (p, 0, 0)),
            pl.BlockSpec((1, suffix_rows), lambda p, j, t: (0, 0)),
            pl.BlockSpec((1, suffix_rows), lambda p, j, t: (0, 0)),
            pl.BlockSpec((suffix_rows, HEAD_SIZE), lambda p, j, t: (0, 0)),
            pl.BlockSpec((suffix_rows, HEAD_SIZE), lambda p, j, t: (0, 0)),
        ]
        + [slot_spec(i) for i in range(PAGES_PER_STEP)],
        out_specs=pl.BlockSpec((1, PAGE_TOKENS, rows // PAGE_TOKENS * HEAD_SIZE), lambda p, j, t: (p, 0, 0)),
        scratch_shapes=[
            pltpu.VMEM((rows, PREFIX_PAGES * PAGE_TOKENS), jnp.float32),
            pltpu.VMEM((PREFIX_PAGES * PAGE_TOKENS, HEAD_SIZE), jnp.bfloat16),
            pltpu.VMEM((HEAD_SIZE // 128, 128, 128), jnp.float32),
        ],
    )
    keys_total = PREFIX_PAGES * PAGE_TOKENS + suffix_rows
    flops = pages * rows * keys_total * HEAD_SIZE * 4
    bytes_accessed = pages * (PREFIX_PAGES * PAGE_TOKENS * 2 * HEAD_SIZE * 2 + rows * HEAD_SIZE * 4)
    return pl.pallas_call(
        page_attention_kernel,
        grid_spec=grid_spec,
        out_shape=jax.ShapeDtypeStruct((pages, PAGE_TOKENS, rows // PAGE_TOKENS * HEAD_SIZE), jnp.bfloat16),
        compiler_params=pltpu.CompilerParams(
            dimension_semantics=("arbitrary", "arbitrary"), vmem_limit_bytes=48 * 1024 * 1024
        ),
        cost_estimate=pl.CostEstimate(
            flops=flops, transcendentals=pages * rows * keys_total, bytes_accessed=bytes_accessed
        ),
    )(table, q, row_req, row_pos, key_req, key_pos, suffix_keys, suffix_values, *([slot_pages] * PAGES_PER_STEP))


def local(
    tokens,
    in_gain,
    w_query,
    key_projection_weight,
    value_projection_weight,
    q_gain,
    k_gain,
    w_out,
    post_gain,
    laurel_left,
    laurel_right,
    laurel_gain,
    prefix_key_slots,
    prefix_value_slots,
    prefix_slot_map,
    page_lengths,
    request_group,
    suffix_page_map,
):
    tok_count = tokens.shape[0]
    pages_here = tok_count // PAGE_TOKENS
    device = lax.axis_index("page")
    first_index = device * tok_count
    prefix_both = jnp.concatenate([prefix_key_slots, prefix_value_slots], axis=1)
    every_slot = lax.all_gather(prefix_both, "page", axis=0, tiled=True)
    requests, position, groups = token_places(first_index, tok_count, page_lengths, request_group)
    normed, queries, fresh_key_rows, fresh_value_rows = project(
        tokens,
        in_gain,
        w_query,
        key_projection_weight,
        value_projection_weight,
        q_gain,
        k_gain,
        position + PREFIX_TOKENS,
    )
    local_slot = suffix_page_map - device * pages_here
    placing = (local_slot[:, None] == jnp.arange(pages_here, dtype=jnp.int32)[None, :]).astype(
        jnp.bfloat16
    )
    both_pages = jnp.concatenate(
        [
            fresh_key_rows.reshape(pages_here, PAGE_TOKENS * HEAD_SIZE),
            fresh_value_rows.reshape(pages_here, PAGE_TOKENS * HEAD_SIZE),
        ],
        axis=1,
    )
    placed = jnp.dot(placing.T, both_pages, preferred_element_type=jnp.float32).astype(jnp.bfloat16)
    suffix_key_cache = placed[:, : PAGE_TOKENS * HEAD_SIZE].reshape(tok_count, HEAD_SIZE)
    suffix_value_cache = placed[:, PAGE_TOKENS * HEAD_SIZE :].reshape(tok_count, HEAD_SIZE)

    reach = (MAXP + pages_here - 2) // pages_here
    fresh_both = jnp.concatenate([fresh_key_rows, fresh_value_rows], axis=1)
    window = fresh_both
    covered = 1
    while covered < reach + 1:
        step = min(covered, reach + 1 - covered)
        moved = passed_along(window[: step * tok_count], "page", covered)
        window = jnp.concatenate([window, moved], axis=0)
        covered += step
    window_requests = []
    window_positions = []
    for shift_step in range(reach + 1):
        far_requests, far_position, _ = token_places(
            first_index - shift_step * tok_count, tok_count, page_lengths, request_group
        )
        window_requests.append(far_requests)
        window_positions.append(far_position)
    key_requests = jnp.concatenate(window_requests, axis=0)
    key_positions = jnp.concatenate(window_positions, axis=0)
    suffix_keys = window[:, :HEAD_SIZE]
    suffix_values = window[:, HEAD_SIZE:]

    heads = queries.shape[1]
    page_queries = queries.reshape(pages_here, PAGE_TOKENS, heads, HEAD_SIZE)
    page_requests = requests.reshape(pages_here, PAGE_TOKENS)
    page_positions = position.reshape(pages_here, PAGE_TOKENS)
    page_groups = groups.reshape(pages_here, PAGE_TOKENS)[:, 0]
    chosen = jnp.take(
        prefix_slot_map.reshape(PREFIX_COUNT, PREFIX_PAGES), page_groups, axis=0
    )
    slot_pages = every_slot.reshape(-1, PAGE_TOKENS, 2 * HEAD_SIZE)
    heads_rows = PAGE_TOKENS * heads
    kv_index = lax.axis_index("kv")
    model_width = tokens.shape[1]
    half_width = model_width // lax.axis_size("kv")

    def columns(source):
        return lax.dynamic_slice_in_dim(source, kv_index * half_width, half_width, source.ndim - 1)

    low_rank = jnp.dot(normed, laurel_left, preferred_element_type=jnp.float32).astype(jnp.bfloat16)
    laurel_full = jnp.dot(low_rank, laurel_right, preferred_element_type=jnp.float32)
    laurel = columns(normed).astype(jnp.float32) + columns(laurel_full) * rms_scale(
        laurel_full
    ) * columns(laurel_gain)
    resident = columns(tokens).astype(jnp.float32) + laurel
    flat_queries = page_queries.reshape(pages_here, heads_rows, HEAD_SIZE)
    row_requests = jnp.repeat(page_requests, heads, axis=1)[..., None]
    row_positions = jnp.repeat(page_positions, heads, axis=1)[..., None]
    (
        resident, suffix_key_cache, suffix_value_cache, flat_queries,
        row_requests, row_positions, suffix_keys, suffix_values,
    ) = lax.optimization_barrier(
        (
            resident, suffix_key_cache, suffix_value_cache, flat_queries,
            row_requests, row_positions, suffix_keys, suffix_values,
        )
    )
    attended = page_attention(
        chosen,
        flat_queries,
        row_requests,
        row_positions,
        key_requests[None, :],
        key_positions[None, :],
        suffix_keys,
        suffix_values,
        slot_pages,
    ).reshape(tok_count, -1)
    attn_part = jnp.dot(attended, w_out, preferred_element_type=jnp.float32)
    partner_part = lax.ppermute(attn_part.astype(jnp.bfloat16), "kv", [(0, 1), (1, 0)])
    summed_out = attn_part + partner_part.astype(jnp.float32)
    attn_branch = columns(summed_out) * rms_scale(summed_out) * columns(post_gain)
    layer_out = ((resident + attn_branch) * 2.0 ** (-0.5)).astype(jnp.bfloat16)
    return (layer_out, suffix_key_cache, suffix_value_cache)


def solution(mesh):
    placed = (
        P("page", None),
        P(),
        P(None, "kv"),
        P(None, "kv"),
        P(None, "kv"),
        P(),
        P(),
        P("kv", None),
        P(),
        P(),
        P(),
        P(),
        P("page", "kv"),
        P("page", "kv"),
        P(),
        P(),
        P(),
        P("page"),
    )
    return jax.shard_map(
        local,
        mesh=mesh,
        in_specs=placed,
        out_specs=(P("page", "kv"), P("page", "kv"), P("page", "kv")),
        check_vma=False,
    )
```

```python
import jax
import jax.numpy as jnp
from jax import lax
from jax.sharding import PartitionSpec as P
from jax.experimental import pallas as pl
from jax.experimental.pallas import tpu as pltpu

HEAD_SIZE = 256
PAGE_TOKENS = 128
PREFIX_TOKENS = 4096
PREFIX_COUNT = 4
MAXP = 8
PREFIX_PAGES = 32


epsilon = 1e-06
rope_base = 1000000.0
masked_low = -1e30


def passed_along(block, axis, distance):
    devices = range(lax.axis_size(axis))
    route = [(i - distance, i) for i in devices if i - distance in devices]
    return lax.ppermute(block, axis, route)


def rms_scale(values):
    return lax.rsqrt(jnp.mean(values * values, axis=-1, keepdims=True) + epsilon)


def rotate(values, positions):
    half_dim = values.shape[-1] // 2
    inv_freq = rope_base ** (-(jnp.arange(half_dim).astype(jnp.float32) * 2.0 / values.shape[-1]))
    angles = positions.astype(jnp.float32)[:, None] * inv_freq[None, :]
    cosine = jnp.cos(angles)[:, None, :]
    sines = jnp.sin(angles)[:, None, :]
    first_half = values[..., :half_dim]
    second_half = values[..., half_dim:]
    return jnp.concatenate(
        [first_half * cosine - second_half * sines, second_half * cosine + first_half * sines],
        axis=-1,
    )


def project(
    tokens,
    in_gain,
    w_query,
    key_projection_weight,
    value_projection_weight,
    q_gain,
    k_gain,
    positions,
):
    tok_count = tokens.shape[0]
    tokens_wide = tokens.astype(jnp.float32)
    normed = (tokens_wide * rms_scale(tokens_wide) * in_gain).astype(jnp.bfloat16)
    queries = jnp.dot(normed, w_query, preferred_element_type=jnp.float32).reshape(
        tok_count, -1, HEAD_SIZE
    )
    queries = rotate(queries * rms_scale(queries) * q_gain, positions).astype(jnp.bfloat16)
    fresh_key_rows = jnp.dot(
        normed, key_projection_weight, preferred_element_type=jnp.float32
    ).reshape(tok_count, -1, HEAD_SIZE)
    fresh_key_rows = rotate(fresh_key_rows * rms_scale(fresh_key_rows) * k_gain, positions).astype(
        jnp.bfloat16
    )
    fresh_value_rows = jnp.dot(
        normed, value_projection_weight, preferred_element_type=jnp.float32
    ).reshape(tok_count, -1, HEAD_SIZE)
    fresh_value_rows = (fresh_value_rows * rms_scale(fresh_value_rows)).astype(jnp.bfloat16)
    return (
        normed,
        queries,
        fresh_key_rows.reshape(tok_count, HEAD_SIZE),
        fresh_value_rows.reshape(tok_count, HEAD_SIZE),
    )


def token_places(first_index, tok_count, page_lengths, request_group):
    tok_ids = first_index + jnp.arange(tok_count, dtype=jnp.int32)
    page_of = tok_ids // PAGE_TOKENS
    page_starts = jnp.cumsum(page_lengths) - page_lengths
    belongs = (page_of[:, None] >= page_starts[None, :]) & (
        page_of[:, None] < (page_starts + page_lengths)[None, :]
    )
    belongs = (belongs & (tok_ids[:, None] >= 0)).astype(jnp.int32)
    request_ids = jnp.arange(page_starts.shape[0], dtype=jnp.int32)
    requests = jnp.sum(belongs * request_ids[None, :], axis=1) - (1 - jnp.sum(belongs, axis=1))
    position = tok_ids - jnp.sum(belongs * page_starts[None, :], axis=1) * PAGE_TOKENS
    groups = jnp.sum(belongs * request_group[None, :], axis=1)
    return (requests, position, groups)


def attend(queries, keys_block, values_block, key_mask):
    scores = jnp.einsum("qhd,kd->qhk", queries, keys_block, preferred_element_type=jnp.float32)
    wide_mask = key_mask[:, None, :]
    scores = jnp.where(wide_mask, scores, masked_low)
    row_top = jnp.max(scores, axis=-1)
    weights = jnp.where(wide_mask, jnp.exp(scores - row_top[..., None]), 0.0)
    row_total = jnp.sum(weights, axis=-1)
    mixture = jnp.einsum(
        "qhk,kd->qhd",
        weights.astype(jnp.bfloat16),
        values_block,
        preferred_element_type=jnp.float32,
    )
    return (row_top, row_total, mixture)


def combine(carried, incoming):
    row_top = jnp.maximum(carried[0], incoming[0])
    old_factor = jnp.exp(carried[0] - row_top)
    new_factor = jnp.exp(incoming[0] - row_top)
    row_total = carried[1] * old_factor + incoming[1] * new_factor
    mixture = carried[2] * old_factor[..., None] + incoming[2] * new_factor[..., None]
    return (row_top, row_total, mixture)


PAGES_PER_STEP = 8


def page_attention_kernel(
    table_ref, q_ref, row_req_ref, row_pos_ref, key_req_ref, key_pos_ref,
    suffix_keys_ref, suffix_values_ref, *rest,
):
    slot_refs = rest[:PAGES_PER_STEP]
    out_ref = rest[PAGES_PER_STEP]
    scores_buf, values_buf = rest[PAGES_PER_STEP + 1 :]
    step = pl.program_id(1)
    last = pl.num_programs(1) - 1
    contract_last = (((1,), (1,)), ((), ()))

    @pl.when(step < last)
    def _():
        q = q_ref[0]
        for i in range(PAGES_PER_STEP):
            page = slot_refs[i][0]
            at = pl.multiple_of((step * PAGES_PER_STEP + i) * PAGE_TOKENS, PAGE_TOKENS)
            scores_buf[:, pl.ds(at, PAGE_TOKENS)] = lax.dot_general(
                q, page[:, :HEAD_SIZE], contract_last, preferred_element_type=jnp.float32
            )
            values_buf[pl.ds(at, PAGE_TOKENS), :] = page[:, HEAD_SIZE:]

    @pl.when(step == last)
    def _():
        rows = q_ref.shape[1]
        chunk = 128
        for r in range(0, rows, chunk):
            q = q_ref[0, r : r + chunk, :]
            mask = (row_req_ref[0, r : r + chunk, :] == key_req_ref[...]) & (
                key_pos_ref[...] <= row_pos_ref[0, r : r + chunk, :]
            )
            suffix_scores = lax.dot_general(
                q, suffix_keys_ref[...], contract_last, preferred_element_type=jnp.float32
            )
            suffix_scores = jnp.where(mask, suffix_scores, masked_low)
            prefix_scores = scores_buf[r : r + chunk, :]
            row_top = jnp.maximum(
                jnp.max(prefix_scores, axis=1, keepdims=True),
                jnp.max(suffix_scores, axis=1, keepdims=True),
            )
            prefix_weights = jnp.exp(prefix_scores - row_top)
            suffix_weights = jnp.where(mask, jnp.exp(suffix_scores - row_top), 0.0)
            row_total = jnp.sum(prefix_weights, axis=1, keepdims=True) + jnp.sum(
                suffix_weights, axis=1, keepdims=True
            )
            mixture = jnp.dot(
                prefix_weights.astype(jnp.bfloat16), values_buf[...],
                preferred_element_type=jnp.float32,
            ) + jnp.dot(
                suffix_weights.astype(jnp.bfloat16), suffix_values_ref[...],
                preferred_element_type=jnp.float32,
            )
            out_ref[0, r : r + chunk, :] = (mixture / row_total).astype(out_ref.dtype)


def page_attention(table, q, row_req, row_pos, key_req, key_pos, suffix_keys, suffix_values, slot_pages):
    pages, rows, _ = q.shape
    steps = PREFIX_PAGES // PAGES_PER_STEP
    suffix_rows = suffix_keys.shape[0]

    def slot_spec(i):
        return pl.BlockSpec(
            (1, PAGE_TOKENS, 2 * HEAD_SIZE),
            lambda p, j, t, i=i: (t[p, jnp.minimum(j * PAGES_PER_STEP + i, PREFIX_PAGES - 1)], 0, 0),
        )

    grid_spec = pltpu.PrefetchScalarGridSpec(
        num_scalar_prefetch=1,
        grid=(pages, steps + 1),
        in_specs=[
            pl.BlockSpec((1, rows, HEAD_SIZE), lambda p, j, t: (p, 0, 0)),
            pl.BlockSpec((1, rows, 1), lambda p, j, t: (p, 0, 0)),
            pl.BlockSpec((1, rows, 1), lambda p, j, t: (p, 0, 0)),
            pl.BlockSpec((1, suffix_rows), lambda p, j, t: (0, 0)),
            pl.BlockSpec((1, suffix_rows), lambda p, j, t: (0, 0)),
            pl.BlockSpec((suffix_rows, HEAD_SIZE), lambda p, j, t: (0, 0)),
            pl.BlockSpec((suffix_rows, HEAD_SIZE), lambda p, j, t: (0, 0)),
        ]
        + [slot_spec(i) for i in range(PAGES_PER_STEP)],
        out_specs=pl.BlockSpec((1, rows, HEAD_SIZE), lambda p, j, t: (p, 0, 0)),
        scratch_shapes=[
            pltpu.VMEM((rows, PREFIX_PAGES * PAGE_TOKENS), jnp.float32),
            pltpu.VMEM((PREFIX_PAGES * PAGE_TOKENS, HEAD_SIZE), jnp.bfloat16),
        ],
    )
    keys_total = PREFIX_PAGES * PAGE_TOKENS + suffix_rows
    flops = pages * rows * keys_total * HEAD_SIZE * 4
    bytes_accessed = pages * (PREFIX_PAGES * PAGE_TOKENS * 2 * HEAD_SIZE * 2 + rows * HEAD_SIZE * 4)
    return pl.pallas_call(
        page_attention_kernel,
        grid_spec=grid_spec,
        out_shape=jax.ShapeDtypeStruct((pages, rows, HEAD_SIZE), jnp.bfloat16),
        compiler_params=pltpu.CompilerParams(
            dimension_semantics=("arbitrary", "arbitrary"), vmem_limit_bytes=48 * 1024 * 1024
        ),
        cost_estimate=pl.CostEstimate(
            flops=flops, transcendentals=pages * rows * keys_total, bytes_accessed=bytes_accessed
        ),
    )(table, q, row_req, row_pos, key_req, key_pos, suffix_keys, suffix_values, *([slot_pages] * PAGES_PER_STEP))


def local(
    tokens,
    in_gain,
    w_query,
    key_projection_weight,
    value_projection_weight,
    q_gain,
    k_gain,
    w_out,
    post_gain,
    laurel_left,
    laurel_right,
    laurel_gain,
    prefix_key_slots,
    prefix_value_slots,
    prefix_slot_map,
    page_lengths,
    request_group,
    suffix_page_map,
):
    tok_count = tokens.shape[0]
    pages_here = tok_count // PAGE_TOKENS
    device = lax.axis_index("page")
    first_index = device * tok_count
    prefix_both = jnp.concatenate([prefix_key_slots, prefix_value_slots], axis=1)
    every_slot = lax.all_gather(prefix_both, "page", axis=0, tiled=True)
    requests, position, groups = token_places(first_index, tok_count, page_lengths, request_group)
    normed, queries, fresh_key_rows, fresh_value_rows = project(
        tokens,
        in_gain,
        w_query,
        key_projection_weight,
        value_projection_weight,
        q_gain,
        k_gain,
        position + PREFIX_TOKENS,
    )
    local_slot = suffix_page_map - device * pages_here
    placing = (local_slot[:, None] == jnp.arange(pages_here, dtype=jnp.int32)[None, :]).astype(
        jnp.bfloat16
    )
    both_pages = jnp.concatenate(
        [
            fresh_key_rows.reshape(pages_here, PAGE_TOKENS * HEAD_SIZE),
            fresh_value_rows.reshape(pages_here, PAGE_TOKENS * HEAD_SIZE),
        ],
        axis=1,
    )
    placed = jnp.dot(placing.T, both_pages, preferred_element_type=jnp.float32).astype(jnp.bfloat16)
    suffix_key_cache = placed[:, : PAGE_TOKENS * HEAD_SIZE].reshape(tok_count, HEAD_SIZE)
    suffix_value_cache = placed[:, PAGE_TOKENS * HEAD_SIZE :].reshape(tok_count, HEAD_SIZE)

    reach = (MAXP + pages_here - 2) // pages_here
    fresh_both = jnp.concatenate([fresh_key_rows, fresh_value_rows], axis=1)
    window = fresh_both
    covered = 1
    while covered < reach + 1:
        step = min(covered, reach + 1 - covered)
        moved = passed_along(window[: step * tok_count], "page", covered)
        window = jnp.concatenate([window, moved], axis=0)
        covered += step
    window_requests = []
    window_positions = []
    for shift_step in range(reach + 1):
        far_requests, far_position, _ = token_places(
            first_index - shift_step * tok_count, tok_count, page_lengths, request_group
        )
        window_requests.append(far_requests)
        window_positions.append(far_position)
    key_requests = jnp.concatenate(window_requests, axis=0)
    key_positions = jnp.concatenate(window_positions, axis=0)
    suffix_keys = window[:, :HEAD_SIZE]
    suffix_values = window[:, HEAD_SIZE:]

    heads = queries.shape[1]
    page_queries = queries.reshape(pages_here, PAGE_TOKENS, heads, HEAD_SIZE)
    page_requests = requests.reshape(pages_here, PAGE_TOKENS)
    page_positions = position.reshape(pages_here, PAGE_TOKENS)
    page_groups = groups.reshape(pages_here, PAGE_TOKENS)[:, 0]
    chosen = jnp.take(
        prefix_slot_map.reshape(PREFIX_COUNT, PREFIX_PAGES), page_groups, axis=0
    )
    slot_pages = every_slot.reshape(-1, PAGE_TOKENS, 2 * HEAD_SIZE)
    heads_rows = PAGE_TOKENS * heads
    kv_index = lax.axis_index("kv")
    model_width = tokens.shape[1]
    half_width = model_width // lax.axis_size("kv")

    def columns(source):
        return lax.dynamic_slice_in_dim(source, kv_index * half_width, half_width, source.ndim - 1)

    low_rank = jnp.dot(normed, laurel_left, preferred_element_type=jnp.float32).astype(jnp.bfloat16)
    laurel_full = jnp.dot(low_rank, laurel_right, preferred_element_type=jnp.float32)
    laurel = columns(normed).astype(jnp.float32) + columns(laurel_full) * rms_scale(
        laurel_full
    ) * columns(laurel_gain)
    resident = columns(tokens).astype(jnp.float32) + laurel
    flat_queries = page_queries.reshape(pages_here, heads_rows, HEAD_SIZE)
    resident, suffix_key_cache, suffix_value_cache, flat_queries = lax.optimization_barrier(
        (resident, suffix_key_cache, suffix_value_cache, flat_queries)
    )
    attended = page_attention(
        chosen,
        flat_queries,
        jnp.repeat(page_requests, heads, axis=1)[..., None],
        jnp.repeat(page_positions, heads, axis=1)[..., None],
        key_requests[None, :],
        key_positions[None, :],
        suffix_keys,
        suffix_values,
        slot_pages,
    ).reshape(tok_count, -1)
    attn_part = jnp.dot(attended, w_out, preferred_element_type=jnp.float32)
    swap = [(0, 1), (1, 0)]
    partner_cols = lax.dynamic_slice_in_dim(attn_part, (1 - kv_index) * half_width, half_width, 1)
    received = lax.ppermute(partner_cols.astype(jnp.bfloat16), "kv", swap)
    summed_half = columns(attn_part) + received.astype(jnp.float32)
    squares_here = jnp.sum(summed_half * summed_half, axis=-1)
    squares_there = lax.ppermute(squares_here, "kv", swap)
    attn_scale = lax.rsqrt((squares_here + squares_there) / model_width + epsilon)[:, None]
    attn_branch = summed_half * attn_scale * columns(post_gain)
    layer_out = ((resident + attn_branch) * 2.0 ** (-0.5)).astype(jnp.bfloat16)
    return (layer_out, suffix_key_cache, suffix_value_cache)


def solution(mesh):
    placed = (
        P("page", None),
        P(),
        P(None, "kv"),
        P(None, "kv"),
        P(None, "kv"),
        P(),
        P(),
        P("kv", None),
        P(),
        P(),
        P(),
        P(),
        P("page", "kv"),
        P("page", "kv"),
        P(),
        P(),
        P(),
        P("page"),
    )
    return jax.shard_map(
        local,
        mesh=mesh,
        in_specs=placed,
        out_specs=(P("page", "kv"), P("page", "kv"), P("page", "kv")),
        check_vma=False,
    )
```
